256 devices in a mesh: seq: 32 (over z, x), head: 8 (over y, core).
Axes of the slice: x: 4, y: 4, z: 8, core: 2. Of those that a mesh axis runs over, the one named last changes fastest.
Arguments:
- queries: bfloat16 [16384, 4096], P('seq', 'head'), may hold values from -6 to 6
- key_rows: bfloat16 [16384, 4096], P('seq', 'head'), may hold values from -6 to 6
- value_rows: bfloat16 [16384, 4096], P('seq', 'head'), may hold values from -18 to 18
- out_grad: bfloat16 [16384, 4096], P('seq', 'head'), may hold values from -6 to 6
- log_decay: float32 [32, 16384], P('head', 'seq'), may hold values from -0.6 to 0
Outputs:
- query_gradient: bfloat16 [16384, 4096], P('seq', 'head')
- key_grad: bfloat16 [16384, 4096], P('seq', 'head')
- value_grad: bfloat16 [16384, 4096], P('seq', 'head')
The draws below stay inside these ranges and needn't reach their ends.
All inputs are finite; a program needn't handle non-finite values.
Results may differ from the reference program's by a relative error of at most 0.006.
Values sent between devices are 32-bit elements; how exact they have to be, the bound alone decides.
No kernel may reach another device: no remote copies, remote signals or barrier semaphores. Data moves between devices by JAX's collectives and lax.ppermute only.
A program may use at most 64 MiB of HBM per device.

```python
import jax
import jax.numpy as jnp
from jax import lax

HEAD_COUNT = 32
DH = 128
BLOCK = 128
TOKEN_COUNT = 16384


def draw_log_decay(key, part):
    key_sequence = jax.random.split(key, 6)
    fast_share = 0.5
    fast_heads = jax.random.bernoulli(key_sequence[0], fast_share, (HEAD_COUNT,))
    fast_rate = jnp.exp(jax.random.uniform(key_sequence[1], (HEAD_COUNT,), jnp.float32, jnp.log(1.0 / 50.0), jnp.log(1.0 / 30.0)))
    slow_rate = jax.random.uniform(key_sequence[2], (HEAD_COUNT,), jnp.float32, 0.05, 0.4) / TOKEN_COUNT
    head_rate = jnp.where(fast_heads, fast_rate, slow_rate)
    factor = jnp.exp(jax.random.uniform(key_sequence[3], (HEAD_COUNT, TOKEN_COUNT), jnp.float32, jnp.log(0.5), jnp.log(2.0)))
    decay_logarithm = -head_rate[:, None] * factor
    spike_positions = jax.random.randint(key_sequence[4], (3,), 0, TOKEN_COUNT)
    token_positions = jnp.arange(TOKEN_COUNT, dtype=jnp.int32)
    spike_selected = jnp.any(token_positions[None, :] == spike_positions[:, None], axis=0)
    spike_retained = jax.random.uniform(key_sequence[5], (HEAD_COUNT, TOKEN_COUNT), jnp.float32, 0.55, 0.8)
    decay_logarithm = jnp.where(spike_selected[None, :], jnp.log(spike_retained), decay_logarithm)
    return decay_logarithm.astype(jnp.float32)


def draw_value_rows(key, part):
    key_sequence = jax.random.split(key, 2)
    head_scale = jnp.exp(jax.random.uniform(key_sequence[0], (HEAD_COUNT,), jnp.float32, jnp.log(0.3), jnp.log(3.0)))
    column_scale = jnp.repeat(head_scale, DH)
    base = jnp.clip(jax.random.normal(key_sequence[1], (TOKEN_COUNT, HEAD_COUNT * DH), jnp.float32), -6.0, 6.0)
    return (base * column_scale[None, :]).astype(jnp.bfloat16)


def level_of(own_key, extent, shards, least, high):
    gain, own = 1.0, jax.random.fold_in(own_key, 6)
    for axis_at, shards_of in shards:
        draws = jnp.exp(jax.random.uniform(jax.random.fold_in(own, axis_at), (shards_of,), jnp.float32, least / len(shards), high / len(shards)))
        gain = gain * jnp.repeat(draws, extent[axis_at] // shards_of).reshape([-1 if axis == axis_at else 1 for axis in range(len(extent))])
    return gain


def normal_values(rng, extent, spread, reach, cuts=(), kind=jnp.bfloat16):
    result = jax.random.normal(rng, extent, jnp.float32) * spread
    if len(cuts) > 0:
        result = level_of(rng, extent, cuts, -0.22, 0.18) * result
    return jnp.clip(result, min=-reach, max=reach).astype(kind)


def setup_inputs(seed: int = 0) -> dict:
    key_list = jax.random.split(jax.random.key(seed), 6)
    queries = normal_values(key_list[0], (TOKEN_COUNT, HEAD_COUNT * DH), 1.0, 6.0, ((0, 32), (1, 8)))
    key_rows = normal_values(key_list[1], (TOKEN_COUNT, HEAD_COUNT * DH), 1.0, 6.0, ((0, 32), (1, 8)))
    value_rows = draw_value_rows(jax.random.fold_in(key_list[5], 71), 0)
    out_grad = normal_values(key_list[3], (TOKEN_COUNT, HEAD_COUNT * DH), 1.0, 6.0, ((0, 32), (1, 8)))
    log_decay = draw_log_decay(jax.random.fold_in(key_list[5], 71), 0)
    return {"queries": queries, "key_rows": key_rows, "value_rows": value_rows, "out_grad": out_grad, "log_decay": log_decay}


epsilon = 1e-06

def rounded(array):
    return lax.optimization_barrier(array.astype(jnp.bfloat16)).astype(jnp.float32)

def pairwise_product(form, left, right):
    return jnp.einsum(form, left, right, precision=lax.Precision.HIGHEST)

def advance(running, block_item):
    block_total, block_term = block_item
    return (jnp.exp(block_total) * running + block_term, running)

def head_columns(array, head_id):
    blocks = TOKEN_COUNT // BLOCK
    column = (head_id * DH).astype(jnp.int32)
    picked = lax.dynamic_slice_in_dim(array, column, DH, 1)
    return picked.astype(jnp.float32).reshape(blocks, BLOCK, DH)

def head_parts(head_id, queries, key_rows, value_rows, log_decay):
    blocks = TOKEN_COUNT // BLOCK
    query_block_rows = head_columns(queries, head_id)
    key_blocks = head_columns(key_rows, head_id)
    value_block_rows = head_columns(value_rows, head_id)
    decay_row = lax.dynamic_index_in_dim(log_decay, head_id, 0, keepdims=False).reshape(blocks, BLOCK)
    inside_block_mask = jnp.cumsum(decay_row, axis=1)
    totals = inside_block_mask[:, -1]
    token_positions = jnp.arange(BLOCK, dtype=jnp.int32)
    causal = (token_positions[:, None] >= token_positions[None, :]).astype(jnp.float32)
    exponent = inside_block_mask[:, :, None] - inside_block_mask[:, None, :]
    decay_mask = jnp.exp(jnp.minimum(exponent, 0.0)) * causal
    scores = pairwise_product('nid,njd->nij', query_block_rows, key_blocks)
    attention_weights = rounded(scores * decay_mask)
    to_end = jnp.exp(totals[:, None] - inside_block_mask)
    keys_scaled = rounded(to_end[:, :, None] * key_blocks)
    block_terms = pairwise_product('njd,nje->nde', keys_scaled, value_block_rows)
    empty_state = jnp.zeros((DH, DH), jnp.float32)
    final_state, states = lax.scan(advance, empty_state, (totals, block_terms))
    backward_state = rounded(states)
    attention_output = pairwise_product('nij,njd->nid', attention_weights, value_block_rows)
    attention_output = attention_output + jnp.exp(inside_block_mask)[:, :, None] * pairwise_product('hrk,hkc->hrc', query_block_rows, backward_state)
    return (query_block_rows, key_blocks, value_block_rows, inside_block_mask, totals, decay_mask, attention_weights, backward_state, to_end, attention_output)

def reference(queries, key_rows, value_rows, out_grad, log_decay):
    head_ids = jnp.arange(HEAD_COUNT, dtype=jnp.int32)
    total_width = HEAD_COUNT * DH

    def head_stats(head_id):
        parts = head_parts(head_id, queries, key_rows, value_rows, log_decay)
        attention_output = parts[-1]
        grad_blocks = head_columns(out_grad, head_id)
        return (lax.optimization_barrier(jnp.sum(attention_output * attention_output, axis=2)), lax.optimization_barrier(jnp.sum(grad_blocks * attention_output, axis=2)))
    squares, crosses = lax.map(head_stats, head_ids)
    inv_rms = lax.rsqrt(lax.optimization_barrier(jnp.sum(squares, axis=0)) / total_width + epsilon)
    mean_cross = inv_rms * lax.optimization_barrier(jnp.sum(crosses, axis=0)) / total_width

    def head_grads(head_id):
        parts = head_parts(head_id, queries, key_rows, value_rows, log_decay)
        query_block_rows, key_blocks, value_block_rows, inside_block_mask, totals, decay_mask, attention_weights, backward_state, to_end, attention_output = parts
        grad_blocks = head_columns(out_grad, head_id)
        normed = attention_output * inv_rms[:, :, None]
        attention_gradient = rounded(inv_rms[:, :, None] * (grad_blocks - normed * mean_cross[:, :, None]))
        score_gradient = pairwise_product('spa,soa->spo', attention_gradient, value_block_rows)
        grad_probs = rounded(score_gradient * decay_mask)
        query_gradient = pairwise_product('nij,njd->nid', grad_probs, key_blocks)
        query_gradient = query_gradient + jnp.exp(inside_block_mask)[:, :, None] * pairwise_product('tjg,tog->tjo', attention_gradient, backward_state)
        key_intra = pairwise_product('nij,nid->njd', grad_probs, query_block_rows)
        value_within_block = pairwise_product('osx,osg->oxg', attention_weights, attention_gradient)
        scaled_query_rows = rounded(jnp.exp(inside_block_mask)[:, :, None] * query_block_rows)
        backward_terms = pairwise_product('gjh,gjb->ghb', scaled_query_rows, attention_gradient)
        empty_state = jnp.zeros((DH, DH), jnp.float32)
        final_state, back_states = lax.scan(advance, empty_state, (totals, backward_terms), reverse=True)
        back_b = rounded(back_states)
        key_grad = key_intra + to_end[:, :, None] * pairwise_product('nje,nde->njd', value_block_rows, back_b)
        value_grad = value_within_block + to_end[:, :, None] * pairwise_product('njd,nde->nje', key_blocks, back_b)
        return (query_gradient.reshape(TOKEN_COUNT, DH).astype(jnp.bfloat16), key_grad.reshape(TOKEN_COUNT, DH).astype(jnp.bfloat16), value_grad.reshape(TOKEN_COUNT, DH).astype(jnp.bfloat16))
    query_all, key_all, value_all = lax.map(head_grads, head_ids)

    def arrange(stacked):
        return jnp.transpose(stacked, (1, 0, 2)).reshape(TOKEN_COUNT, HEAD_COUNT * DH)
    return (arrange(query_all), arrange(key_all), arrange(value_all))
```

```python
import jax
import jax.numpy as jnp
from jax import lax
from jax.sharding import PartitionSpec as P

HEAD_COUNT = 32
DH = 128
BLOCK = 128


epsilon = 1e-06
highest = lax.Precision.HIGHEST


def pack(total, state):
    row = jnp.broadcast_to(total[:, None, None], (state.shape[0], 1, state.shape[2]))
    return jnp.concatenate([state, row], axis=1)


def unpack(payload):
    rows = payload.shape[1] - 1
    return payload[:, rows, 0], payload[:, :rows, :]


def forward_scan(total, state, ranks):
    win_a, win_b = total, state
    excl_a, excl_b = jnp.zeros_like(total), jnp.zeros_like(state)
    shift = 1
    while shift < ranks:
        pairs = [(i, i + shift) for i in range(ranks - shift)]
        got_a, got_b = unpack(lax.ppermute(pack(win_a, win_b), "seq", pairs))
        excl_b = jnp.exp(excl_a)[:, None, None] * got_b + excl_b
        excl_a = excl_a + got_a
        if 2 * shift < ranks:
            win_b = jnp.exp(win_a)[:, None, None] * got_b + win_b
            win_a = win_a + got_a
        shift *= 2
    return excl_b


def backward_scan(total, state, ranks):
    win_a, win_c = total, state
    excl_a, excl_c = jnp.zeros_like(total), jnp.zeros_like(state)
    shift = 1
    while shift < ranks:
        pairs = [(i + shift, i) for i in range(ranks - shift)]
        got_a, got_c = unpack(lax.ppermute(pack(win_a, win_c), "seq", pairs))
        excl_c = excl_c + jnp.exp(excl_a)[:, None, None] * got_c
        excl_a = excl_a + got_a
        if 2 * shift < ranks:
            win_c = win_c + jnp.exp(win_a)[:, None, None] * got_c
            win_a = win_a + got_a
        shift *= 2
    return excl_c


def shards(queries, key_rows, value_rows, out_grad, log_decay, seq_ranks):
    tok_rows, row_width = queries.shape
    heads_dev = log_decay.shape[0]
    head_size = row_width // heads_dev
    blocks = tok_rows // BLOCK
    total_width = HEAD_COUNT * DH
    block_shape = (blocks, BLOCK, heads_dev, head_size)
    query_block_rows = queries.reshape(block_shape)
    key_blocks = key_rows.reshape(block_shape)
    value_block_rows = value_rows.reshape(block_shape)
    grad_blocks = out_grad.reshape(block_shape)
    decay_blocks = jnp.transpose(log_decay.reshape(heads_dev, blocks, BLOCK), (1, 2, 0))
    inside_block_mask = jnp.cumsum(decay_blocks, axis=1)
    totals = inside_block_mask[:, -1, :]
    before = jnp.cumsum(totals, axis=0) - totals
    shard_total = jnp.sum(totals, axis=0)
    token_positions = jnp.arange(BLOCK)
    causal = (token_positions[:, None] >= token_positions[None, :]).astype(jnp.float32)
    within_heads = jnp.transpose(inside_block_mask, (0, 2, 1))
    exponent = within_heads[:, :, :, None] - within_heads[:, :, None, :]
    decay_mask = jnp.exp(jnp.minimum(exponent, 0.0)) * causal
    scores = jnp.einsum(
        "nihd,njhd->nhij", query_block_rows, key_blocks, preferred_element_type=jnp.float32
    )
    attention_weights = (scores * decay_mask).astype(jnp.bfloat16)
    intra_out = jnp.einsum(
        "nhij,njhd->nihd", attention_weights, value_block_rows, preferred_element_type=jnp.float32
    )
    to_end = jnp.exp(totals[:, None, :] - inside_block_mask)
    keys_scaled = (to_end[..., None] * key_blocks).astype(jnp.bfloat16)
    block_terms = jnp.einsum(
        "njhd,njhe->nhde", keys_scaled, value_block_rows, preferred_element_type=jnp.float32
    )
    block_ids = jnp.arange(blocks)
    earlier_blocks = (block_ids[:, None] > block_ids[None, :]).astype(jnp.float32)
    forward_exp = before[:, None, :] - before[None, :, :] - totals[None, :, :]
    forward_mix = jnp.exp(jnp.minimum(forward_exp, 0.0)) * earlier_blocks[:, :, None]
    local_states = jnp.einsum("nmh,mhde->nhde", forward_mix, block_terms, precision=highest)
    shard_state = jnp.einsum(
        "mh,mhde->hde",
        jnp.exp(shard_total[None, :] - before - totals),
        block_terms,
        precision=highest,
    )
    incoming = forward_scan(shard_total, shard_state, seq_ranks)
    states = local_states + jnp.exp(before)[:, :, None, None] * incoming[None]
    backward_state = states.astype(jnp.bfloat16)
    inter_out = jnp.einsum(
        "nihd,nhde->nihe", query_block_rows, backward_state, preferred_element_type=jnp.float32
    )
    attention_output = intra_out + jnp.exp(inside_block_mask)[..., None] * inter_out
    grad_f32 = grad_blocks.astype(jnp.float32)
    square = jnp.sum(attention_output * attention_output, axis=(2, 3))
    cross_raw = jnp.sum(grad_f32 * attention_output, axis=(2, 3))
    stats = lax.psum(jnp.stack([square, cross_raw]), "head")
    inv_rms = lax.rsqrt(stats[0] / total_width + epsilon)
    mean_cross = inv_rms * stats[1] / total_width
    normed = attention_output * inv_rms[:, :, None, None]
    attention_gradient = (
        inv_rms[:, :, None, None]
        * (grad_f32 - normed * mean_cross[:, :, None, None])
    ).astype(jnp.bfloat16)
    score_gradient = jnp.einsum(
        "nihe,njhe->nhij", attention_gradient, value_block_rows, preferred_element_type=jnp.float32
    )
    grad_probs = (score_gradient * decay_mask).astype(jnp.bfloat16)
    query_gradient = jnp.einsum(
        "nhij,njhd->nihd", grad_probs, key_blocks, preferred_element_type=jnp.float32
    )
    query_gradient = query_gradient + jnp.exp(inside_block_mask)[..., None] * jnp.einsum(
        "nihe,nhde->nihd", attention_gradient, backward_state, preferred_element_type=jnp.float32
    )
    key_intra = jnp.einsum(
        "nhij,nihd->njhd", grad_probs, query_block_rows, preferred_element_type=jnp.float32
    )
    value_within_block = jnp.einsum(
        "nhij,nihe->njhe", attention_weights, attention_gradient, preferred_element_type=jnp.float32
    )
    scaled_query_rows = (jnp.exp(inside_block_mask)[..., None] * query_block_rows).astype(
        jnp.bfloat16
    )
    backward_terms = jnp.einsum(
        "nihd,nihe->nhde", scaled_query_rows, attention_gradient, preferred_element_type=jnp.float32
    )
    later_blocks = (block_ids[:, None] < block_ids[None, :]).astype(jnp.float32)
    backward_exp = before[None, :, :] - before[:, None, :] - totals[:, None, :]
    backward_mix = jnp.exp(jnp.minimum(backward_exp, 0.0)) * later_blocks[:, :, None]
    local_back = jnp.einsum("nmh,mhde->nhde", backward_mix, backward_terms, precision=highest)
    shard_back = jnp.einsum("mh,mhde->hde", jnp.exp(before), backward_terms, precision=highest)
    later_state = backward_scan(shard_total, shard_back, seq_ranks)
    back_states = (
        local_back
        + jnp.exp(shard_total[None, :] - before - totals)[:, :, None, None] * later_state[None]
    )
    back_b = back_states.astype(jnp.bfloat16)
    key_grad = key_intra + to_end[..., None] * jnp.einsum(
        "njhe,nhde->njhd", value_block_rows, back_b, preferred_element_type=jnp.float32
    )
    value_grad = value_within_block + to_end[..., None] * jnp.einsum(
        "njhd,nhde->njhe", key_blocks, back_b, preferred_element_type=jnp.float32
    )
    return (
        query_gradient.reshape(tok_rows, row_width).astype(jnp.bfloat16),
        key_grad.reshape(tok_rows, row_width).astype(jnp.bfloat16),
        value_grad.reshape(tok_rows, row_width).astype(jnp.bfloat16),
    )


def solution(mesh):
    seq_ranks = mesh.shape["seq"]

    def body(queries, key_rows, value_rows, out_grad, log_decay):
        return shards(queries, key_rows, value_rows, out_grad, log_decay, seq_ranks)

    return jax.shard_map(
        body,
        mesh=mesh,
        in_specs=(
            P("seq", "head"),
            P("seq", "head"),
            P("seq", "head"),
            P("seq", "head"),
            P("head", "seq"),
        ),
        out_specs=(P("seq", "head"), P("seq", "head"), P("seq", "head")),
        check_vma=False,
    )
```

```python
import jax
import jax.numpy as jnp
from jax import lax
from jax.sharding import Mesh, PartitionSpec as P

HEAD_COUNT = 32
DH = 128
BLOCK = 128
ROW = 4


epsilon = 1e-06
highest = lax.Precision.HIGHEST


def pack(total, state):
    row = jnp.broadcast_to(total[:, None, None], (state.shape[0], 1, state.shape[2]))
    return jnp.concatenate([state, row], axis=1)


def unpack(payload):
    rows = payload.shape[1] - 1
    return payload[:, rows, 0], payload[:, :rows, :]


def forward_scan(total, state, axis, ranks):
    win_a, win_b = total, state
    excl_a, excl_b = jnp.zeros_like(total), jnp.zeros_like(state)
    shift = 1
    while shift < ranks:
        pairs = [(i, i + shift) for i in range(ranks - shift)]
        got_a, got_b = unpack(lax.ppermute(pack(win_a, win_b), axis, pairs))
        excl_b = jnp.exp(excl_a)[:, None, None] * got_b + excl_b
        excl_a = excl_a + got_a
        if 2 * shift < ranks:
            win_b = jnp.exp(win_a)[:, None, None] * got_b + win_b
            win_a = win_a + got_a
        shift *= 2
    return excl_b


def backward_scan(total, state, axis, ranks):
    win_a, win_c = total, state
    excl_a, excl_c = jnp.zeros_like(total), jnp.zeros_like(state)
    shift = 1
    while shift < ranks:
        pairs = [(i + shift, i) for i in range(ranks - shift)]
        got_a, got_c = unpack(lax.ppermute(pack(win_a, win_c), axis, pairs))
        excl_c = excl_c + jnp.exp(excl_a)[:, None, None] * got_c
        excl_a = excl_a + got_a
        if 2 * shift < ranks:
            win_c = win_c + jnp.exp(win_a)[:, None, None] * got_c
            win_a = win_a + got_a
        shift *= 2
    return excl_c


def exchange(payload, axis, ranks):
    me = lax.axis_index(axis)
    got = [lax.dynamic_index_in_dim(payload, me, 0, keepdims=False)]
    for shift in range(1, ranks):
        send = lax.dynamic_index_in_dim(payload, (me + shift) % ranks, 0, keepdims=False)
        pairs = [(i, (i + shift) % ranks) for i in range(ranks)]
        got.append(lax.ppermute(send, axis, pairs))
    stacked = jnp.stack(got)
    order = (me - jnp.arange(ranks)) % ranks
    return jnp.take(stacked, order, axis=0)


def incoming_states(shard_total, shard_state, row_ranks, col_ranks):
    parts = exchange(pack(shard_total, shard_state), "sx", row_ranks)
    part_a, part_b = parts[:, -1, 0], parts[:, :-1, :]
    run_a = jnp.zeros((), jnp.float32)
    run_b = jnp.zeros_like(part_b[0])
    row_a, row_b = [], []
    for pos in range(row_ranks):
        row_a.append(run_a)
        row_b.append(run_b)
        run_b = jnp.exp(part_a[pos]) * run_b + part_b[pos]
        run_a = run_a + part_a[pos]
    before_row = forward_scan(run_a[None], run_b[None], "sz", col_ranks)[0]
    result = jnp.stack(
        [jnp.exp(row_a[pos]) * before_row + row_b[pos] for pos in range(row_ranks)]
    )
    return exchange(result, "sx", row_ranks)


def outgoing_states(shard_total, shard_back, row_ranks, col_ranks):
    parts = exchange(pack(shard_total, shard_back), "sx", row_ranks)
    part_a, part_c = parts[:, -1, 0], parts[:, :-1, :]
    run_a = jnp.zeros((), jnp.float32)
    run_c = jnp.zeros_like(part_c[0])
    row_a, row_c = [None] * row_ranks, [None] * row_ranks
    for pos in reversed(range(row_ranks)):
        row_a[pos] = run_a
        row_c[pos] = run_c
        run_c = part_c[pos] + jnp.exp(part_a[pos]) * run_c
        run_a = run_a + part_a[pos]
    after_row = backward_scan(run_a[None], run_c[None], "sz", col_ranks)[0]
    result = jnp.stack(
        [row_c[pos] + jnp.exp(row_a[pos]) * after_row for pos in range(row_ranks)]
    )
    return exchange(result, "sx", row_ranks)


def head_sum(values, ranks):
    gathered = exchange(jnp.broadcast_to(values[None], (ranks,) + values.shape), "head", ranks)
    return jnp.sum(gathered, axis=0)


def shards(queries, key_rows, value_rows, out_grad, log_decay, row_ranks, col_ranks, head_ranks):
    tok_rows, row_width = queries.shape
    heads_dev = log_decay.shape[0]
    head_size = row_width // heads_dev
    blocks = tok_rows // BLOCK
    total_width = HEAD_COUNT * DH
    block_shape = (blocks, BLOCK, heads_dev, head_size)
    query_block_rows = queries.reshape(block_shape)
    key_blocks = key_rows.reshape(block_shape)
    value_block_rows = value_rows.reshape(block_shape)
    grad_blocks = out_grad.reshape(block_shape)
    decay_blocks = jnp.transpose(log_decay.reshape(heads_dev, blocks, BLOCK), (1, 2, 0))
    inside_block_mask = jnp.cumsum(decay_blocks, axis=1)
    totals = inside_block_mask[:, -1, :]
    before = jnp.cumsum(totals, axis=0) - totals
    shard_total = jnp.sum(totals, axis=0)
    token_positions = jnp.arange(BLOCK)
    causal = (token_positions[:, None] >= token_positions[None, :]).astype(jnp.float32)
    within_heads = jnp.transpose(inside_block_mask, (0, 2, 1))
    exponent = within_heads[:, :, :, None] - within_heads[:, :, None, :]
    decay_mask = jnp.exp(jnp.minimum(exponent, 0.0)) * causal
    scores = jnp.einsum(
        "nihd,njhd->nhij", query_block_rows, key_blocks, preferred_element_type=jnp.float32
    )
    attention_weights = (scores * decay_mask).astype(jnp.bfloat16)
    intra_out = jnp.einsum(
        "nhij,njhd->nihd", attention_weights, value_block_rows, preferred_element_type=jnp.float32
    )
    to_end = jnp.exp(totals[:, None, :] - inside_block_mask)
    keys_scaled = (to_end[..., None] * key_blocks).astype(jnp.bfloat16)
    block_terms = jnp.einsum(
        "njhd,njhe->nhde", keys_scaled, value_block_rows, preferred_element_type=jnp.float32
    )
    block_ids = jnp.arange(blocks)
    earlier_blocks = (block_ids[:, None] > block_ids[None, :]).astype(jnp.float32)
    forward_exp = before[:, None, :] - before[None, :, :] - totals[None, :, :]
    forward_mix = jnp.exp(jnp.minimum(forward_exp, 0.0)) * earlier_blocks[:, :, None]
    local_states = jnp.einsum("nmh,mhde->nhde", forward_mix, block_terms, precision=highest)
    shard_state = jnp.einsum(
        "mh,mhde->hde",
        jnp.exp(shard_total[None, :] - before - totals),
        block_terms,
        precision=highest,
    )
    incoming = incoming_states(shard_total, shard_state, row_ranks, col_ranks)
    states = local_states + jnp.exp(before)[:, :, None, None] * incoming[None]
    backward_state = states.astype(jnp.bfloat16)
    inter_out = jnp.einsum(
        "nihd,nhde->nihe", query_block_rows, backward_state, preferred_element_type=jnp.float32
    )
    attention_output = intra_out + jnp.exp(inside_block_mask)[..., None] * inter_out
    grad_f32 = grad_blocks.astype(jnp.float32)
    square = jnp.sum(attention_output * attention_output, axis=(2, 3))
    cross_raw = jnp.sum(grad_f32 * attention_output, axis=(2, 3))
    stats = head_sum(jnp.stack([square, cross_raw]), head_ranks)
    inv_rms = lax.rsqrt(stats[0] / total_width + epsilon)
    mean_cross = inv_rms * stats[1] / total_width
    normed = attention_output * inv_rms[:, :, None, None]
    attention_gradient = (
        inv_rms[:, :, None, None]
        * (grad_f32 - normed * mean_cross[:, :, None, None])
    ).astype(jnp.bfloat16)
    score_gradient = jnp.einsum(
        "nihe,njhe->nhij", attention_gradient, value_block_rows, preferred_element_type=jnp.float32
    )
    grad_probs = (score_gradient * decay_mask).astype(jnp.bfloat16)
    query_gradient = jnp.einsum(
        "nhij,njhd->nihd", grad_probs, key_blocks, preferred_element_type=jnp.float32
    )
    query_gradient = query_gradient + jnp.exp(inside_block_mask)[..., None] * jnp.einsum(
        "nihe,nhde->nihd", attention_gradient, backward_state, preferred_element_type=jnp.float32
    )
    key_intra = jnp.einsum(
        "nhij,nihd->njhd", grad_probs, query_block_rows, preferred_element_type=jnp.float32
    )
    value_within_block = jnp.einsum(
        "nhij,nihe->njhe", attention_weights, attention_gradient, preferred_element_type=jnp.float32
    )
    scaled_query_rows = (jnp.exp(inside_block_mask)[..., None] * query_block_rows).astype(
        jnp.bfloat16
    )
    backward_terms = jnp.einsum(
        "nihd,nihe->nhde", scaled_query_rows, attention_gradient, preferred_element_type=jnp.float32
    )
    later_blocks = (block_ids[:, None] < block_ids[None, :]).astype(jnp.float32)
    backward_exp = before[None, :, :] - before[:, None, :] - totals[:, None, :]
    backward_mix = jnp.exp(jnp.minimum(backward_exp, 0.0)) * later_blocks[:, :, None]
    local_back = jnp.einsum("nmh,mhde->nhde", backward_mix, backward_terms, precision=highest)
    shard_back = jnp.einsum("mh,mhde->hde", jnp.exp(before), backward_terms, precision=highest)
    later_state = outgoing_states(shard_total, shard_back, row_ranks, col_ranks)
    back_states = (
        local_back
        + jnp.exp(shard_total[None, :] - before - totals)[:, :, None, None] * later_state[None]
    )
    back_b = back_states.astype(jnp.bfloat16)
    key_grad = key_intra + to_end[..., None] * jnp.einsum(
        "njhe,nhde->njhd", value_block_rows, back_b, preferred_element_type=jnp.float32
    )
    value_grad = value_within_block + to_end[..., None] * jnp.einsum(
        "njhd,nhde->njhe", key_blocks, back_b, preferred_element_type=jnp.float32
    )
    return (
        query_gradient.reshape(tok_rows, row_width).astype(jnp.bfloat16),
        key_grad.reshape(tok_rows, row_width).astype(jnp.bfloat16),
        value_grad.reshape(tok_rows, row_width).astype(jnp.bfloat16),
    )


def solution(mesh):
    seq_ranks = mesh.shape["seq"]
    head_ranks = mesh.shape["head"]
    row_ranks = ROW if seq_ranks % ROW == 0 else 1
    col_ranks = seq_ranks // row_ranks
    grid = Mesh(mesh.devices.reshape(col_ranks, row_ranks, head_ranks), ("sz", "sx", "head"))

    def body(queries, key_rows, value_rows, out_grad, log_decay):
        return shards(
            queries, key_rows, value_rows, out_grad, log_decay, row_ranks, col_ranks, head_ranks
        )

    rows = P(("sz", "sx"), "head")
    return jax.shard_map(
        body,
        mesh=grid,
        in_specs=(rows, rows, rows, rows, P("head", ("sz", "sx"))),
        out_specs=(rows, rows, rows),
        check_vma=False,
    )
```

```python
import jax
import jax.numpy as jnp
from jax import lax
from jax.sharding import Mesh, PartitionSpec as P

HEAD_COUNT = 32
DH = 128
BLOCK = 128
ROW = 4


epsilon = 1e-06
highest = lax.Precision.HIGHEST


def pack(total, state):
    row = jnp.broadcast_to(total[:, None, None], (state.shape[0], 1, state.shape[2]))
    return jnp.concatenate([state, row], axis=1)


def unpack(payload):
    rows = payload.shape[1] - 1
    return payload[:, rows, 0], payload[:, :rows, :]


def forward_scan(total, state, axis, ranks):
    win_a, win_b = total, state
    excl_a, excl_b = jnp.zeros_like(total), jnp.zeros_like(state)
    shift = 1
    while shift < ranks:
        pairs = [(i, i + shift) for i in range(ranks - shift)]
        got_a, got_b = unpack(lax.ppermute(pack(win_a, win_b), axis, pairs))
        excl_b = jnp.exp(excl_a)[:, None, None] * got_b + excl_b
        excl_a = excl_a + got_a
        if 2 * shift < ranks:
            win_b = jnp.exp(win_a)[:, None, None] * got_b + win_b
            win_a = win_a + got_a
        shift *= 2
    return excl_b


def backward_scan(total, state, axis, ranks):
    win_a, win_c = total, state
    excl_a, excl_c = jnp.zeros_like(total), jnp.zeros_like(state)
    shift = 1
    while shift < ranks:
        pairs = [(i + shift, i) for i in range(ranks - shift)]
        got_a, got_c = unpack(lax.ppermute(pack(win_a, win_c), axis, pairs))
        excl_c = excl_c + jnp.exp(excl_a)[:, None, None] * got_c
        excl_a = excl_a + got_a
        if 2 * shift < ranks:
            win_c = win_c + jnp.exp(win_a)[:, None, None] * got_c
            win_a = win_a + got_a
        shift *= 2
    return excl_c


def exchange(payload, axis, ranks):
    me = lax.axis_index(axis)
    got = [lax.dynamic_index_in_dim(payload, me, 0, keepdims=False)]
    for shift in range(1, ranks):
        send = lax.dynamic_index_in_dim(payload, (me + shift) % ranks, 0, keepdims=False)
        pairs = [(i, (i + shift) % ranks) for i in range(ranks)]
        got.append(lax.ppermute(send, axis, pairs))
    stacked = jnp.stack(got)
    order = (me - jnp.arange(ranks)) % ranks
    return jnp.take(stacked, order, axis=0)


def column_forward(total, state, axis, ranks):
    rows = state.shape[0] // ranks
    pieces = pack(jnp.broadcast_to(total, (ranks,)), state.reshape(ranks, rows, state.shape[1]))
    got = lax.all_to_all(pieces, axis, 0, 0, tiled=True)
    got_a, got_b = unpack(got)
    run = jnp.zeros_like(got_b[0])
    outs = []
    for k in range(ranks):
        outs.append(run)
        run = jnp.exp(got_a[k]) * run + got_b[k]
    back = lax.all_to_all(jnp.stack(outs), axis, 0, 0, tiled=True)
    return back.reshape(state.shape)


def column_backward(total, state, axis, ranks):
    rows = state.shape[0] // ranks
    pieces = pack(jnp.broadcast_to(total, (ranks,)), state.reshape(ranks, rows, state.shape[1]))
    got = lax.all_to_all(pieces, axis, 0, 0, tiled=True)
    got_a, got_c = unpack(got)
    run = jnp.zeros_like(got_c[0])
    outs = [None] * ranks
    for k in reversed(range(ranks)):
        outs[k] = run
        run = got_c[k] + jnp.exp(got_a[k]) * run
    back = lax.all_to_all(jnp.stack(outs), axis, 0, 0, tiled=True)
    return back.reshape(state.shape)


def incoming_states(shard_total, shard_state, row_ranks, col_ranks):
    parts = exchange(pack(shard_total, shard_state), "sx", row_ranks)
    part_a, part_b = parts[:, -1, 0], parts[:, :-1, :]
    run_a = jnp.zeros((), jnp.float32)
    run_b = jnp.zeros_like(part_b[0])
    row_a, row_b = [], []
    for pos in range(row_ranks):
        row_a.append(run_a)
        row_b.append(run_b)
        run_b = jnp.exp(part_a[pos]) * run_b + part_b[pos]
        run_a = run_a + part_a[pos]
    before_row = column_forward(run_a, run_b, "sz", col_ranks)
    result = jnp.stack(
        [jnp.exp(row_a[pos]) * before_row + row_b[pos] for pos in range(row_ranks)]
    )
    return exchange(result, "sx", row_ranks)


def outgoing_states(shard_total, shard_back, row_ranks, col_ranks):
    parts = exchange(pack(shard_total, shard_back), "sx", row_ranks)
    part_a, part_c = parts[:, -1, 0], parts[:, :-1, :]
    run_a = jnp.zeros((), jnp.float32)
    run_c = jnp.zeros_like(part_c[0])
    row_a, row_c = [None] * row_ranks, [None] * row_ranks
    for pos in reversed(range(row_ranks)):
        row_a[pos] = run_a
        row_c[pos] = run_c
        run_c = part_c[pos] + jnp.exp(part_a[pos]) * run_c
        run_a = run_a + part_a[pos]
    after_row = column_backward(run_a, run_c, "sz", col_ranks)
    result = jnp.stack(
        [row_c[pos] + jnp.exp(row_a[pos]) * after_row for pos in range(row_ranks)]
    )
    return exchange(result, "sx", row_ranks)


def head_sum(values, ranks):
    copies = jnp.broadcast_to(values[None], (ranks,) + values.shape)
    gathered = lax.all_to_all(copies, "head", 0, 0, tiled=True)
    return jnp.sum(gathered, axis=0)


def shards(queries, key_rows, value_rows, out_grad, log_decay, row_ranks, col_ranks, head_ranks):
    tok_rows, row_width = queries.shape
    heads_dev = log_decay.shape[0]
    head_size = row_width // heads_dev
    blocks = tok_rows // BLOCK
    total_width = HEAD_COUNT * DH
    block_shape = (blocks, BLOCK, heads_dev, head_size)
    query_block_rows = queries.reshape(block_shape)
    key_blocks = key_rows.reshape(block_shape)
    value_block_rows = value_rows.reshape(block_shape)
    grad_blocks = out_grad.reshape(block_shape)
    decay_blocks = jnp.transpose(log_decay.reshape(heads_dev, blocks, BLOCK), (1, 2, 0))
    inside_block_mask = jnp.cumsum(decay_blocks, axis=1)
    totals = inside_block_mask[:, -1, :]
    before = jnp.cumsum(totals, axis=0) - totals
    shard_total = jnp.sum(totals, axis=0)
    token_positions = jnp.arange(BLOCK)
    causal = (token_positions[:, None] >= token_positions[None, :]).astype(jnp.float32)
    within_heads = jnp.transpose(inside_block_mask, (0, 2, 1))
    exponent = within_heads[:, :, :, None] - within_heads[:, :, None, :]
    decay_mask = jnp.exp(jnp.minimum(exponent, 0.0)) * causal
    scores = jnp.einsum(
        "nihd,njhd->nhij", query_block_rows, key_blocks, preferred_element_type=jnp.float32
    )
    attention_weights = (scores * decay_mask).astype(jnp.bfloat16)
    intra_out = jnp.einsum(
        "nhij,njhd->nihd", attention_weights, value_block_rows, preferred_element_type=jnp.float32
    )
    to_end = jnp.exp(totals[:, None, :] - inside_block_mask)
    keys_scaled = (to_end[..., None] * key_blocks).astype(jnp.bfloat16)
    block_terms = jnp.einsum(
        "njhd,njhe->nhde", keys_scaled, value_block_rows, preferred_element_type=jnp.float32
    )
    block_ids = jnp.arange(blocks)
    earlier_blocks = (block_ids[:, None] > block_ids[None, :]).astype(jnp.float32)
    forward_exp = before[:, None, :] - before[None, :, :] - totals[None, :, :]
    forward_mix = jnp.exp(jnp.minimum(forward_exp, 0.0)) * earlier_blocks[:, :, None]
    local_states = jnp.einsum("nmh,mhde->nhde", forward_mix, block_terms, precision=highest)
    shard_state = jnp.einsum(
        "mh,mhde->hde",
        jnp.exp(shard_total[None, :] - before - totals),
        block_terms,
        precision=highest,
    )
    incoming = incoming_states(shard_total, shard_state, row_ranks, col_ranks)
    states = local_states + jnp.exp(before)[:, :, None, None] * incoming[None]
    backward_state = states.astype(jnp.bfloat16)
    inter_out = jnp.einsum(
        "nihd,nhde->nihe", query_block_rows, backward_state, preferred_element_type=jnp.float32
    )
    attention_output = intra_out + jnp.exp(inside_block_mask)[..., None] * inter_out
    grad_f32 = grad_blocks.astype(jnp.float32)
    square = jnp.sum(attention_output * attention_output, axis=(2, 3))
    cross_raw = jnp.sum(grad_f32 * attention_output, axis=(2, 3))
    stats = head_sum(jnp.stack([square, cross_raw]), head_ranks)
    inv_rms = lax.rsqrt(stats[0] / total_width + epsilon)
    mean_cross = inv_rms * stats[1] / total_width
    normed = attention_output * inv_rms[:, :, None, None]
    attention_gradient = (
        inv_rms[:, :, None, None]
        * (grad_f32 - normed * mean_cross[:, :, None, None])
    ).astype(jnp.bfloat16)
    score_gradient = jnp.einsum(
        "nihe,njhe->nhij", attention_gradient, value_block_rows, preferred_element_type=jnp.float32
    )
    grad_probs = (score_gradient * decay_mask).astype(jnp.bfloat16)
    query_gradient = jnp.einsum(
        "nhij,njhd->nihd", grad_probs, key_blocks, preferred_element_type=jnp.float32
    )
    query_gradient = query_gradient + jnp.exp(inside_block_mask)[..., None] * jnp.einsum(
        "nihe,nhde->nihd", attention_gradient, backward_state, preferred_element_type=jnp.float32
    )
    key_intra = jnp.einsum(
        "nhij,nihd->njhd", grad_probs, query_block_rows, preferred_element_type=jnp.float32
    )
    value_within_block = jnp.einsum(
        "nhij,nihe->njhe", attention_weights, attention_gradient, preferred_element_type=jnp.float32
    )
    scaled_query_rows = (jnp.exp(inside_block_mask)[..., None] * query_block_rows).astype(
        jnp.bfloat16
    )
    backward_terms = jnp.einsum(
        "nihd,nihe->nhde", scaled_query_rows, attention_gradient, preferred_element_type=jnp.float32
    )
    later_blocks = (block_ids[:, None] < block_ids[None, :]).astype(jnp.float32)
    backward_exp = before[None, :, :] - before[:, None, :] - totals[:, None, :]
    backward_mix = jnp.exp(jnp.minimum(backward_exp, 0.0)) * later_blocks[:, :, None]
    local_back = jnp.einsum("nmh,mhde->nhde", backward_mix, backward_terms, precision=highest)
    shard_back = jnp.einsum("mh,mhde->hde", jnp.exp(before), backward_terms, precision=highest)
    later_state = outgoing_states(shard_total, shard_back, row_ranks, col_ranks)
    back_states = (
        local_back
        + jnp.exp(shard_total[None, :] - before - totals)[:, :, None, None] * later_state[None]
    )
    back_b = back_states.astype(jnp.bfloat16)
    key_grad = key_intra + to_end[..., None] * jnp.einsum(
        "njhe,nhde->njhd", value_block_rows, back_b, preferred_element_type=jnp.float32
    )
    value_grad = value_within_block + to_end[..., None] * jnp.einsum(
        "njhd,nhde->njhe", key_blocks, back_b, preferred_element_type=jnp.float32
    )
    return (
        query_gradient.reshape(tok_rows, row_width).astype(jnp.bfloat16),
        key_grad.reshape(tok_rows, row_width).astype(jnp.bfloat16),
        value_grad.reshape(tok_rows, row_width).astype(jnp.bfloat16),
    )


def solution(mesh):
    seq_ranks = mesh.shape["seq"]
    head_ranks = mesh.shape["head"]
    row_ranks = ROW if seq_ranks % ROW == 0 else 1
    col_ranks = seq_ranks // row_ranks
    grid = Mesh(mesh.devices.reshape(col_ranks, row_ranks, head_ranks), ("sz", "sx", "head"))

    def body(queries, key_rows, value_rows, out_grad, log_decay):
        return shards(
            queries, key_rows, value_rows, out_grad, log_decay, row_ranks, col_ranks, head_ranks
        )

    rows = P(("sz", "sx"), "head")
    return jax.shard_map(
        body,
        mesh=grid,
        in_specs=(rows, rows, rows, rows, P("head", ("sz", "sx"))),
        out_specs=(rows, rows, rows),
        check_vma=False,
    )
```

```python
import jax
import jax.numpy as jnp
from jax import lax
from jax.sharding import Mesh, PartitionSpec as P

HEAD_COUNT = 32
DH = 128
BLOCK = 128
ROW = 4


epsilon = 1e-06
highest = lax.Precision.HIGHEST


def pack(total_row, state):
    return jnp.concatenate([state, total_row], axis=1)


def unpack(payload):
    return payload[:, -1:, :], payload[:, :-1, :]


def forward_scan(total, state, axis, ranks):
    win_a, win_b = total, state
    excl_a, excl_b = jnp.zeros_like(total), jnp.zeros_like(state)
    shift = 1
    while shift < ranks:
        pairs = [(i, i + shift) for i in range(ranks - shift)]
        got_a, got_b = unpack(lax.ppermute(pack(win_a, win_b), axis, pairs))
        excl_b = jnp.exp(excl_a) * got_b + excl_b
        excl_a = excl_a + got_a
        if 2 * shift < ranks:
            win_b = jnp.exp(win_a) * got_b + win_b
            win_a = win_a + got_a
        shift *= 2
    return excl_b


def backward_scan(total, state, axis, ranks):
    win_a, win_c = total, state
    excl_a, excl_c = jnp.zeros_like(total), jnp.zeros_like(state)
    shift = 1
    while shift < ranks:
        pairs = [(i + shift, i) for i in range(ranks - shift)]
        got_a, got_c = unpack(lax.ppermute(pack(win_a, win_c), axis, pairs))
        excl_c = excl_c + jnp.exp(excl_a) * got_c
        excl_a = excl_a + got_a
        if 2 * shift < ranks:
            win_c = win_c + jnp.exp(win_a) * got_c
            win_a = win_a + got_a
        shift *= 2
    return excl_c


def exchange(payload, axis, ranks):
    me = lax.axis_index(axis)
    got = [lax.dynamic_index_in_dim(payload, me, 0, keepdims=False)]
    for shift in range(1, ranks):
        send = lax.dynamic_index_in_dim(payload, (me + shift) % ranks, 0, keepdims=False)
        pairs = [(i, (i + shift) % ranks) for i in range(ranks)]
        got.append(lax.ppermute(send, axis, pairs))
    stacked = jnp.stack(got)
    order = (me - jnp.arange(ranks)) % ranks
    return jnp.take(stacked, order, axis=0)


def lane_rows(shard_total, width):
    return jnp.broadcast_to(shard_total[:, None, None], (shard_total.shape[0], 1, width))


def incoming_states(shard_total, shard_state, row_ranks, col_ranks):
    parts = exchange(pack(lane_rows(shard_total, shard_state.shape[2]), shard_state), "sx", row_ranks)
    part_a, part_b = unpack(parts)
    run_a = jnp.zeros_like(part_a[0])
    run_b = jnp.zeros_like(part_b[0])
    row_a, row_b = [], []
    for pos in range(row_ranks):
        row_a.append(run_a)
        row_b.append(run_b)
        run_b = jnp.exp(part_a[pos]) * run_b + part_b[pos]
        run_a = run_a + part_a[pos]
    before_row = forward_scan(run_a[None], run_b[None], "sz", col_ranks)[0]
    result = jnp.stack(
        [jnp.exp(row_a[pos]) * before_row + row_b[pos] for pos in range(row_ranks)]
    )
    return exchange(result, "sx", row_ranks)


def outgoing_states(shard_total, shard_back, row_ranks, col_ranks):
    parts = exchange(pack(lane_rows(shard_total, shard_back.shape[2]), shard_back), "sx", row_ranks)
    part_a, part_c = unpack(parts)
    run_a = jnp.zeros_like(part_a[0])
    run_c = jnp.zeros_like(part_c[0])
    row_a, row_c = [None] * row_ranks, [None] * row_ranks
    for pos in reversed(range(row_ranks)):
        row_a[pos] = run_a
        row_c[pos] = run_c
        run_c = part_c[pos] + jnp.exp(part_a[pos]) * run_c
        run_a = run_a + part_a[pos]
    after_row = backward_scan(run_a[None], run_c[None], "sz", col_ranks)[0]
    result = jnp.stack(
        [row_c[pos] + jnp.exp(row_a[pos]) * after_row for pos in range(row_ranks)]
    )
    return exchange(result, "sx", row_ranks)


def head_sum(values, ranks):
    copies = jnp.broadcast_to(values[None], (ranks,) + values.shape)
    gathered = lax.all_to_all(copies, "head", 0, 0, tiled=True)
    return jnp.sum(gathered, axis=0)


def shards(queries, key_rows, value_rows, out_grad, log_decay, row_ranks, col_ranks, head_ranks):
    tok_rows, row_width = queries.shape
    heads_dev = log_decay.shape[0]
    head_size = row_width // heads_dev
    blocks = tok_rows // BLOCK
    total_width = HEAD_COUNT * DH
    block_shape = (blocks, BLOCK, heads_dev, head_size)
    query_block_rows = queries.reshape(block_shape)
    key_blocks = key_rows.reshape(block_shape)
    value_block_rows = value_rows.reshape(block_shape)
    grad_blocks = out_grad.reshape(block_shape)
    decay_blocks = jnp.transpose(log_decay.reshape(heads_dev, blocks, BLOCK), (1, 2, 0))
    inside_block_mask = jnp.cumsum(decay_blocks, axis=1)
    totals = inside_block_mask[:, -1, :]
    before = jnp.cumsum(totals, axis=0) - totals
    shard_total = jnp.sum(totals, axis=0)
    token_positions = jnp.arange(BLOCK)
    causal = (token_positions[:, None] >= token_positions[None, :]).astype(jnp.float32)
    within_heads = jnp.transpose(inside_block_mask, (0, 2, 1))
    exponent = within_heads[:, :, :, None] - within_heads[:, :, None, :]
    decay_mask = jnp.exp(jnp.minimum(exponent, 0.0)) * causal
    scores = jnp.einsum(
        "nihd,njhd->nhij", query_block_rows, key_blocks, preferred_element_type=jnp.float32
    )
    attention_weights = (scores * decay_mask).astype(jnp.bfloat16)
    intra_out = jnp.einsum(
        "nhij,njhd->nihd", attention_weights, value_block_rows, preferred_element_type=jnp.float32
    )
    to_end = jnp.exp(totals[:, None, :] - inside_block_mask)
    keys_scaled = (to_end[..., None] * key_blocks).astype(jnp.bfloat16)
    block_terms = jnp.einsum(
        "njhd,njhe->nhde", keys_scaled, value_block_rows, preferred_element_type=jnp.float32
    )
    block_ids = jnp.arange(blocks)
    earlier_blocks = (block_ids[:, None] > block_ids[None, :]).astype(jnp.float32)
    forward_exp = before[:, None, :] - before[None, :, :] - totals[None, :, :]
    forward_mix = jnp.exp(jnp.minimum(forward_exp, 0.0)) * earlier_blocks[:, :, None]
    local_states = jnp.einsum("nmh,mhde->nhde", forward_mix, block_terms, precision=highest)
    shard_state = jnp.einsum(
        "mh,mhde->hde",
        jnp.exp(shard_total[None, :] - before - totals),
        block_terms,
        precision=highest,
    )
    incoming = incoming_states(shard_total, shard_state, row_ranks, col_ranks)
    states = local_states + jnp.exp(before)[:, :, None, None] * incoming[None]
    backward_state = states.astype(jnp.bfloat16)
    inter_out = jnp.einsum(
        "nihd,nhde->nihe", query_block_rows, backward_state, preferred_element_type=jnp.float32
    )
    attention_output = intra_out + jnp.exp(inside_block_mask)[..., None] * inter_out
    grad_f32 = grad_blocks.astype(jnp.float32)
    square = jnp.sum(attention_output * attention_output, axis=(2, 3))
    cross_raw = jnp.sum(grad_f32 * attention_output, axis=(2, 3))
    stats = head_sum(jnp.stack([square, cross_raw]), head_ranks)
    inv_rms = lax.rsqrt(stats[0] / total_width + epsilon)
    mean_cross = inv_rms * stats[1] / total_width
    normed = attention_output * inv_rms[:, :, None, None]
    attention_gradient = (
        inv_rms[:, :, None, None]
        * (grad_f32 - normed * mean_cross[:, :, None, None])
    ).astype(jnp.bfloat16)
    score_gradient = jnp.einsum(
        "nihe,njhe->nhij", attention_gradient, value_block_rows, preferred_element_type=jnp.float32
    )
    grad_probs = (score_gradient * decay_mask).astype(jnp.bfloat16)
    query_gradient = jnp.einsum(
        "nhij,njhd->nihd", grad_probs, key_blocks, preferred_element_type=jnp.float32
    )
    query_gradient = query_gradient + jnp.exp(inside_block_mask)[..., None] * jnp.einsum(
        "nihe,nhde->nihd", attention_gradient, backward_state, preferred_element_type=jnp.float32
    )
    key_intra = jnp.einsum(
        "nhij,nihd->njhd", grad_probs, query_block_rows, preferred_element_type=jnp.float32
    )
    value_within_block = jnp.einsum(
        "nhij,nihe->njhe", attention_weights, attention_gradient, preferred_element_type=jnp.float32
    )
    scaled_query_rows = (jnp.exp(inside_block_mask)[..., None] * query_block_rows).astype(
        jnp.bfloat16
    )
    backward_terms = jnp.einsum(
        "nihd,nihe->nhde", scaled_query_rows, attention_gradient, preferred_element_type=jnp.float32
    )
    later_blocks = (block_ids[:, None] < block_ids[None, :]).astype(jnp.float32)
    backward_exp = before[None, :, :] - before[:, None, :] - totals[:, None, :]
    backward_mix = jnp.exp(jnp.minimum(backward_exp, 0.0)) * later_blocks[:, :, None]
    local_back = jnp.einsum("nmh,mhde->nhde", backward_mix, backward_terms, precision=highest)
    shard_back = jnp.einsum("mh,mhde->hde", jnp.exp(before), backward_terms, precision=highest)
    later_state = outgoing_states(shard_total, shard_back, row_ranks, col_ranks)
    back_states = (
        local_back
        + jnp.exp(shard_total[None, :] - before - totals)[:, :, None, None] * later_state[None]
    )
    back_b = back_states.astype(jnp.bfloat16)
    key_grad = key_intra + to_end[..., None] * jnp.einsum(
        "njhe,nhde->njhd", value_block_rows, back_b, preferred_element_type=jnp.float32
    )
    value_grad = value_within_block + to_end[..., None] * jnp.einsum(
        "njhd,nhde->njhe", key_blocks, back_b, preferred_element_type=jnp.float32
    )
    return (
        query_gradient.reshape(tok_rows, row_width).astype(jnp.bfloat16),
        key_grad.reshape(tok_rows, row_width).astype(jnp.bfloat16),
        value_grad.reshape(tok_rows, row_width).astype(jnp.bfloat16),
    )


def solution(mesh):
    seq_ranks = mesh.shape["seq"]
    head_ranks = mesh.shape["head"]
    row_ranks = ROW if seq_ranks % ROW == 0 else 1
    col_ranks = seq_ranks // row_ranks
    grid = Mesh(mesh.devices.reshape(col_ranks, row_ranks, head_ranks), ("sz", "sx", "head"))

    def body(queries, key_rows, value_rows, out_grad, log_decay):
        return shards(
            queries, key_rows, value_rows, out_grad, log_decay, row_ranks, col_ranks, head_ranks
        )

    rows = P(("sz", "sx"), "head")
    return jax.shard_map(
        body,
        mesh=grid,
        in_specs=(rows, rows, rows, rows, P("head", ("sz", "sx"))),
        out_specs=(rows, rows, rows),
        check_vma=False,
    )
```

```python
import jax
import jax.numpy as jnp
from jax import lax
from jax.sharding import Mesh, PartitionSpec as P

HEAD_COUNT = 32
DH = 128
BLOCK = 128
ROW = 4


epsilon = 1e-06
highest = lax.Precision.HIGHEST


def pack(total_row, state):
    return jnp.concatenate([state, total_row], axis=1)


def unpack(payload):
    return payload[:, -1:, :], payload[:, :-1, :]


def radix_shifts(ranks):
    rounds, width = [], 1
    while width < ranks:
        rounds.append([s for s in (width, 2 * width) if s < ranks])
        width *= 3
    return rounds


def forward_scan(total, state, axis, ranks):
    win_a, win_b = total, state
    excl_a, excl_b = jnp.zeros_like(total), jnp.zeros_like(state)
    rounds = radix_shifts(ranks)
    for step, shifts in enumerate(rounds):
        payload = pack(win_a, win_b)
        got = [
            unpack(lax.ppermute(payload, axis, [(i, i + s) for i in range(ranks - s)]))
            for s in shifts
        ]
        last = step == len(rounds) - 1
        for got_a, got_b in got:
            excl_b = jnp.exp(excl_a) * got_b + excl_b
            excl_a = excl_a + got_a
            if not last:
                win_b = jnp.exp(win_a) * got_b + win_b
                win_a = win_a + got_a
    return excl_b


def backward_scan(total, state, axis, ranks):
    win_a, win_c = total, state
    excl_a, excl_c = jnp.zeros_like(total), jnp.zeros_like(state)
    rounds = radix_shifts(ranks)
    for step, shifts in enumerate(rounds):
        payload = pack(win_a, win_c)
        got = [
            unpack(lax.ppermute(payload, axis, [(i + s, i) for i in range(ranks - s)]))
            for s in shifts
        ]
        last = step == len(rounds) - 1
        for got_a, got_c in got:
            excl_c = excl_c + jnp.exp(excl_a) * got_c
            excl_a = excl_a + got_a
            if not last:
                win_c = win_c + jnp.exp(win_a) * got_c
                win_a = win_a + got_a
    return excl_c


def exchange(payload, axis, ranks):
    me = lax.axis_index(axis)
    got = [lax.dynamic_index_in_dim(payload, me, 0, keepdims=False)]
    for shift in range(1, ranks):
        send = lax.dynamic_index_in_dim(payload, (me + shift) % ranks, 0, keepdims=False)
        pairs = [(i, (i + shift) % ranks) for i in range(ranks)]
        got.append(lax.ppermute(send, axis, pairs))
    stacked = jnp.stack(got)
    order = (me - jnp.arange(ranks)) % ranks
    return jnp.take(stacked, order, axis=0)


def lane_rows(shard_total, width):
    return jnp.broadcast_to(shard_total[:, None, None], (shard_total.shape[0], 1, width))


def incoming_states(shard_total, shard_state, row_ranks, col_ranks):
    parts = exchange(pack(lane_rows(shard_total, shard_state.shape[2]), shard_state), "sx", row_ranks)
    part_a, part_b = unpack(parts)
    run_a = jnp.zeros_like(part_a[0])
    run_b = jnp.zeros_like(part_b[0])
    row_a, row_b = [], []
    for pos in range(row_ranks):
        row_a.append(run_a)
        row_b.append(run_b)
        run_b = jnp.exp(part_a[pos]) * run_b + part_b[pos]
        run_a = run_a + part_a[pos]
    before_row = forward_scan(run_a[None], run_b[None], "sz", col_ranks)[0]
    result = jnp.stack(
        [jnp.exp(row_a[pos]) * before_row + row_b[pos] for pos in range(row_ranks)]
    )
    return exchange(result, "sx", row_ranks)


def outgoing_states(shard_total, shard_back, row_ranks, col_ranks):
    parts = exchange(pack(lane_rows(shard_total, shard_back.shape[2]), shard_back), "sx", row_ranks)
    part_a, part_c = unpack(parts)
    run_a = jnp.zeros_like(part_a[0])
    run_c = jnp.zeros_like(part_c[0])
    row_a, row_c = [None] * row_ranks, [None] * row_ranks
    for pos in reversed(range(row_ranks)):
        row_a[pos] = run_a
        row_c[pos] = run_c
        run_c = part_c[pos] + jnp.exp(part_a[pos]) * run_c
        run_a = run_a + part_a[pos]
    after_row = backward_scan(run_a[None], run_c[None], "sz", col_ranks)[0]
    result = jnp.stack(
        [row_c[pos] + jnp.exp(row_a[pos]) * after_row for pos in range(row_ranks)]
    )
    return exchange(result, "sx", row_ranks)


def head_sum(values, ranks):
    copies = jnp.broadcast_to(values[None], (ranks,) + values.shape)
    gathered = lax.all_to_all(copies, "head", 0, 0, tiled=True)
    return jnp.sum(gathered, axis=0)


def shards(queries, key_rows, value_rows, out_grad, log_decay, row_ranks, col_ranks, head_ranks):
    tok_rows, row_width = queries.shape
    heads_dev = log_decay.shape[0]
    head_size = row_width // heads_dev
    blocks = tok_rows // BLOCK
    total_width = HEAD_COUNT * DH
    block_shape = (blocks, BLOCK, heads_dev, head_size)
    query_block_rows = queries.reshape(block_shape)
    key_blocks = key_rows.reshape(block_shape)
    value_block_rows = value_rows.reshape(block_shape)
    grad_blocks = out_grad.reshape(block_shape)
    decay_blocks = jnp.transpose(log_decay.reshape(heads_dev, blocks, BLOCK), (1, 2, 0))
    inside_block_mask = jnp.cumsum(decay_blocks, axis=1)
    totals = inside_block_mask[:, -1, :]
    before = jnp.cumsum(totals, axis=0) - totals
    shard_total = jnp.sum(totals, axis=0)
    token_positions = jnp.arange(BLOCK)
    causal = (token_positions[:, None] >= token_positions[None, :]).astype(jnp.float32)
    within_heads = jnp.transpose(inside_block_mask, (0, 2, 1))
    exponent = within_heads[:, :, :, None] - within_heads[:, :, None, :]
    decay_mask = jnp.exp(jnp.minimum(exponent, 0.0)) * causal
    scores = jnp.einsum(
        "nihd,njhd->nhij", query_block_rows, key_blocks, preferred_element_type=jnp.float32
    )
    attention_weights = (scores * decay_mask).astype(jnp.bfloat16)
    intra_out = jnp.einsum(
        "nhij,njhd->nihd", attention_weights, value_block_rows, preferred_element_type=jnp.float32
    )
    to_end = jnp.exp(totals[:, None, :] - inside_block_mask)
    keys_scaled = (to_end[..., None] * key_blocks).astype(jnp.bfloat16)
    block_terms = jnp.einsum(
        "njhd,njhe->nhde", keys_scaled, value_block_rows, preferred_element_type=jnp.float32
    )
    block_ids = jnp.arange(blocks)
    earlier_blocks = (block_ids[:, None] > block_ids[None, :]).astype(jnp.float32)
    forward_exp = before[:, None, :] - before[None, :, :] - totals[None, :, :]
    forward_mix = jnp.exp(jnp.minimum(forward_exp, 0.0)) * earlier_blocks[:, :, None]
    local_states = jnp.einsum("nmh,mhde->nhde", forward_mix, block_terms, precision=highest)
    shard_state = jnp.einsum(
        "mh,mhde->hde",
        jnp.exp(shard_total[None, :] - before - totals),
        block_terms,
        precision=highest,
    )
    incoming = incoming_states(shard_total, shard_state, row_ranks, col_ranks)
    states = local_states + jnp.exp(before)[:, :, None, None] * incoming[None]
    backward_state = states.astype(jnp.bfloat16)
    inter_out = jnp.einsum(
        "nihd,nhde->nihe", query_block_rows, backward_state, preferred_element_type=jnp.float32
    )
    attention_output = intra_out + jnp.exp(inside_block_mask)[..., None] * inter_out
    grad_f32 = grad_blocks.astype(jnp.float32)
    square = jnp.sum(attention_output * attention_output, axis=(2, 3))
    cross_raw = jnp.sum(grad_f32 * attention_output, axis=(2, 3))
    stats = head_sum(jnp.stack([square, cross_raw]), head_ranks)
    inv_rms = lax.rsqrt(stats[0] / total_width + epsilon)
    mean_cross = inv_rms * stats[1] / total_width
    normed = attention_output * inv_rms[:, :, None, None]
    attention_gradient = (
        inv_rms[:, :, None, None]
        * (grad_f32 - normed * mean_cross[:, :, None, None])
    ).astype(jnp.bfloat16)
    score_gradient = jnp.einsum(
        "nihe,njhe->nhij", attention_gradient, value_block_rows, preferred_element_type=jnp.float32
    )
    grad_probs = (score_gradient * decay_mask).astype(jnp.bfloat16)
    query_gradient = jnp.einsum(
        "nhij,njhd->nihd", grad_probs, key_blocks, preferred_element_type=jnp.float32
    )
    query_gradient = query_gradient + jnp.exp(inside_block_mask)[..., None] * jnp.einsum(
        "nihe,nhde->nihd", attention_gradient, backward_state, preferred_element_type=jnp.float32
    )
    key_intra = jnp.einsum(
        "nhij,nihd->njhd", grad_probs, query_block_rows, preferred_element_type=jnp.float32
    )
    value_within_block = jnp.einsum(
        "nhij,nihe->njhe", attention_weights, attention_gradient, preferred_element_type=jnp.float32
    )
    scaled_query_rows = (jnp.exp(inside_block_mask)[..., None] * query_block_rows).astype(
        jnp.bfloat16
    )
    backward_terms = jnp.einsum(
        "nihd,nihe->nhde", scaled_query_rows, attention_gradient, preferred_element_type=jnp.float32
    )
    later_blocks = (block_ids[:, None] < block_ids[None, :]).astype(jnp.float32)
    backward_exp = before[None, :, :] - before[:, None, :] - totals[:, None, :]
    backward_mix = jnp.exp(jnp.minimum(backward_exp, 0.0)) * later_blocks[:, :, None]
    local_back = jnp.einsum("nmh,mhde->nhde", backward_mix, backward_terms, precision=highest)
    shard_back = jnp.einsum("mh,mhde->hde", jnp.exp(before), backward_terms, precision=highest)
    later_state = outgoing_states(shard_total, shard_back, row_ranks, col_ranks)
    back_states = (
        local_back
        + jnp.exp(shard_total[None, :] - before - totals)[:, :, None, None] * later_state[None]
    )
    back_b = back_states.astype(jnp.bfloat16)
    key_grad = key_intra + to_end[..., None] * jnp.einsum(
        "njhe,nhde->njhd", value_block_rows, back_b, preferred_element_type=jnp.float32
    )
    value_grad = value_within_block + to_end[..., None] * jnp.einsum(
        "njhd,nhde->njhe", key_blocks, back_b, preferred_element_type=jnp.float32
    )
    return (
        query_gradient.reshape(tok_rows, row_width).astype(jnp.bfloat16),
        key_grad.reshape(tok_rows, row_width).astype(jnp.bfloat16),
        value_grad.reshape(tok_rows, row_width).astype(jnp.bfloat16),
    )


def solution(mesh):
    seq_ranks = mesh.shape["seq"]
    head_ranks = mesh.shape["head"]
    row_ranks = ROW if seq_ranks % ROW == 0 else 1
    col_ranks = seq_ranks // row_ranks
    grid = Mesh(mesh.devices.reshape(col_ranks, row_ranks, head_ranks), ("sz", "sx", "head"))

    def body(queries, key_rows, value_rows, out_grad, log_decay):
        return shards(
            queries, key_rows, value_rows, out_grad, log_decay, row_ranks, col_ranks, head_ranks
        )

    rows = P(("sz", "sx"), "head")
    return jax.shard_map(
        body,
        mesh=grid,
        in_specs=(rows, rows, rows, rows, P("head", ("sz", "sx"))),
        out_specs=(rows, rows, rows),
        check_vma=False,
    )
```

```python
import jax
import jax.numpy as jnp
from jax import lax
from jax.sharding import Mesh, PartitionSpec as P

HEAD_COUNT = 32
DH = 128
BLOCK = 128
ROW = 4


epsilon = 1e-06
highest = lax.Precision.HIGHEST


def pack(total_row, state):
    return jnp.concatenate([state, total_row], axis=1)


def unpack(payload):
    return payload[:, -1:, :], payload[:, :-1, :]


def radix_shifts(ranks):
    rounds, width = [], 1
    while width < ranks:
        rounds.append([s for s in (width, 2 * width) if s < ranks])
        width *= 3
    return rounds


def forward_scan(total, state, axis, ranks):
    win_a, win_b = total, state
    excl_a, excl_b = jnp.zeros_like(total), jnp.zeros_like(state)
    rounds = radix_shifts(ranks)
    for step, shifts in enumerate(rounds):
        payload = pack(win_a, win_b)
        got = [
            unpack(lax.ppermute(payload, axis, [(i, i + s) for i in range(ranks - s)]))
            for s in shifts
        ]
        last = step == len(rounds) - 1
        for got_a, got_b in got:
            excl_b = jnp.exp(excl_a) * got_b + excl_b
            excl_a = excl_a + got_a
            if not last:
                win_b = jnp.exp(win_a) * got_b + win_b
                win_a = win_a + got_a
    return excl_b


def backward_scan(total, state, axis, ranks):
    win_a, win_c = total, state
    excl_a, excl_c = jnp.zeros_like(total), jnp.zeros_like(state)
    rounds = radix_shifts(ranks)
    for step, shifts in enumerate(rounds):
        payload = pack(win_a, win_c)
        got = [
            unpack(lax.ppermute(payload, axis, [(i + s, i) for i in range(ranks - s)]))
            for s in shifts
        ]
        last = step == len(rounds) - 1
        for got_a, got_c in got:
            excl_c = excl_c + jnp.exp(excl_a) * got_c
            excl_a = excl_a + got_a
            if not last:
                win_c = win_c + jnp.exp(win_a) * got_c
                win_a = win_a + got_a
    return excl_c


def exchange(payload, axis, ranks):
    me = lax.axis_index(axis)
    got = [lax.dynamic_index_in_dim(payload, me, 0, keepdims=False)]
    for shift in range(1, ranks):
        send = lax.dynamic_index_in_dim(payload, (me + shift) % ranks, 0, keepdims=False)
        pairs = [(i, (i + shift) % ranks) for i in range(ranks)]
        got.append(lax.ppermute(send, axis, pairs))
    stacked = jnp.stack(got)
    order = (me - jnp.arange(ranks)) % ranks
    return jnp.take(stacked, order, axis=0)


def lane_rows(shard_total, width):
    return jnp.broadcast_to(shard_total[:, None, None], (shard_total.shape[0], 1, width))


def incoming_states(shard_total, shard_state, row_ranks, col_ranks):
    parts = exchange(pack(lane_rows(shard_total, shard_state.shape[2]), shard_state), "sx", row_ranks)
    part_a, part_b = unpack(parts)
    run_a = jnp.zeros_like(part_a[0])
    run_b = jnp.zeros_like(part_b[0])
    row_a, row_b = [], []
    for pos in range(row_ranks):
        row_a.append(run_a)
        row_b.append(run_b)
        run_b = jnp.exp(part_a[pos]) * run_b + part_b[pos]
        run_a = run_a + part_a[pos]
    before_row = forward_scan(run_a[None], run_b[None], "sz", col_ranks)[0]
    result = jnp.stack(
        [jnp.exp(row_a[pos]) * before_row + row_b[pos] for pos in range(row_ranks)]
    )
    return exchange(result, "sx", row_ranks)


def outgoing_states(shard_total, shard_back, row_ranks, col_ranks):
    parts = exchange(pack(lane_rows(shard_total, shard_back.shape[2]), shard_back), "sx", row_ranks)
    part_a, part_c = unpack(parts)
    run_a = jnp.zeros_like(part_a[0])
    run_c = jnp.zeros_like(part_c[0])
    row_a, row_c = [None] * row_ranks, [None] * row_ranks
    for pos in reversed(range(row_ranks)):
        row_a[pos] = run_a
        row_c[pos] = run_c
        run_c = part_c[pos] + jnp.exp(part_a[pos]) * run_c
        run_a = run_a + part_a[pos]
    after_row = backward_scan(run_a[None], run_c[None], "sz", col_ranks)[0]
    result = jnp.stack(
        [row_c[pos] + jnp.exp(row_a[pos]) * after_row for pos in range(row_ranks)]
    )
    return exchange(result, "sx", row_ranks)


def head_sum(values, ranks):
    copies = jnp.broadcast_to(values[None], (ranks,) + values.shape)
    gathered = lax.all_to_all(copies, "head", 0, 0, tiled=True)
    return jnp.sum(gathered, axis=0)


def weigh_blocks(weights, terms):
    return jnp.sum(weights[:, :, None, None] * terms, axis=0)


def mix_blocks(mix, terms):
    return jnp.stack([weigh_blocks(mix[n], terms) for n in range(mix.shape[0])])


def shards(queries, key_rows, value_rows, out_grad, log_decay, row_ranks, col_ranks, head_ranks):
    tok_rows, row_width = queries.shape
    heads_dev = log_decay.shape[0]
    head_size = row_width // heads_dev
    blocks = tok_rows // BLOCK
    total_width = HEAD_COUNT * DH
    block_shape = (blocks, BLOCK, heads_dev, head_size)
    query_block_rows = queries.reshape(block_shape)
    key_blocks = key_rows.reshape(block_shape)
    value_block_rows = value_rows.reshape(block_shape)
    grad_blocks = out_grad.reshape(block_shape)
    decay_blocks = jnp.transpose(log_decay.reshape(heads_dev, blocks, BLOCK), (1, 2, 0))
    inside_block_mask = jnp.cumsum(decay_blocks, axis=1)
    totals = inside_block_mask[:, -1, :]
    before = jnp.cumsum(totals, axis=0) - totals
    shard_total = jnp.sum(totals, axis=0)
    token_positions = jnp.arange(BLOCK)
    causal = (token_positions[:, None] >= token_positions[None, :]).astype(jnp.float32)
    within_heads = jnp.transpose(inside_block_mask, (0, 2, 1))
    exponent = within_heads[:, :, :, None] - within_heads[:, :, None, :]
    decay_mask = jnp.exp(jnp.minimum(exponent, 0.0)) * causal
    scores = jnp.einsum(
        "nihd,njhd->nhij", query_block_rows, key_blocks, preferred_element_type=jnp.float32
    )
    attention_weights = (scores * decay_mask).astype(jnp.bfloat16)
    intra_out = jnp.einsum(
        "nhij,njhd->nihd", attention_weights, value_block_rows, preferred_element_type=jnp.float32
    )
    to_end = jnp.exp(totals[:, None, :] - inside_block_mask)
    keys_scaled = (to_end[..., None] * key_blocks).astype(jnp.bfloat16)
    block_terms = jnp.einsum(
        "njhd,njhe->nhde", keys_scaled, value_block_rows, preferred_element_type=jnp.float32
    )
    block_ids = jnp.arange(blocks)
    earlier_blocks = (block_ids[:, None] > block_ids[None, :]).astype(jnp.float32)
    forward_exp = before[:, None, :] - before[None, :, :] - totals[None, :, :]
    forward_mix = jnp.exp(jnp.minimum(forward_exp, 0.0)) * earlier_blocks[:, :, None]
    local_states = mix_blocks(forward_mix, block_terms)
    shard_state = weigh_blocks(jnp.exp(shard_total[None, :] - before - totals), block_terms)
    incoming = incoming_states(shard_total, shard_state, row_ranks, col_ranks)
    states = local_states + jnp.exp(before)[:, :, None, None] * incoming[None]
    backward_state = states.astype(jnp.bfloat16)
    inter_out = jnp.einsum(
        "nihd,nhde->nihe", query_block_rows, backward_state, preferred_element_type=jnp.float32
    )
    attention_output = intra_out + jnp.exp(inside_block_mask)[..., None] * inter_out
    grad_f32 = grad_blocks.astype(jnp.float32)
    square = jnp.sum(attention_output * attention_output, axis=(2, 3))
    cross_raw = jnp.sum(grad_f32 * attention_output, axis=(2, 3))
    stats = head_sum(jnp.stack([square, cross_raw]), head_ranks)
    inv_rms = lax.rsqrt(stats[0] / total_width + epsilon)
    mean_cross = inv_rms * stats[1] / total_width
    normed = attention_output * inv_rms[:, :, None, None]
    attention_gradient = (
        inv_rms[:, :, None, None]
        * (grad_f32 - normed * mean_cross[:, :, None, None])
    ).astype(jnp.bfloat16)
    score_gradient = jnp.einsum(
        "nihe,njhe->nhij", attention_gradient, value_block_rows, preferred_element_type=jnp.float32
    )
    grad_probs = (score_gradient * decay_mask).astype(jnp.bfloat16)
    query_gradient = jnp.einsum(
        "nhij,njhd->nihd", grad_probs, key_blocks, preferred_element_type=jnp.float32
    )
    query_gradient = query_gradient + jnp.exp(inside_block_mask)[..., None] * jnp.einsum(
        "nihe,nhde->nihd", attention_gradient, backward_state, preferred_element_type=jnp.float32
    )
    key_intra = jnp.einsum(
        "nhij,nihd->njhd", grad_probs, query_block_rows, preferred_element_type=jnp.float32
    )
    value_within_block = jnp.einsum(
        "nhij,nihe->njhe", attention_weights, attention_gradient, preferred_element_type=jnp.float32
    )
    scaled_query_rows = (jnp.exp(inside_block_mask)[..., None] * query_block_rows).astype(
        jnp.bfloat16
    )
    backward_terms = jnp.einsum(
        "nihd,nihe->nhde", scaled_query_rows, attention_gradient, preferred_element_type=jnp.float32
    )
    later_blocks = (block_ids[:, None] < block_ids[None, :]).astype(jnp.float32)
    backward_exp = before[None, :, :] - before[:, None, :] - totals[:, None, :]
    backward_mix = jnp.exp(jnp.minimum(backward_exp, 0.0)) * later_blocks[:, :, None]
    local_back = mix_blocks(backward_mix, backward_terms)
    shard_back = weigh_blocks(jnp.exp(before), backward_terms)
    later_state = outgoing_states(shard_total, shard_back, row_ranks, col_ranks)
    back_states = (
        local_back
        + jnp.exp(shard_total[None, :] - before - totals)[:, :, None, None] * later_state[None]
    )
    back_b = back_states.astype(jnp.bfloat16)
    key_grad = key_intra + to_end[..., None] * jnp.einsum(
        "njhe,nhde->njhd", value_block_rows, back_b, preferred_element_type=jnp.float32
    )
    value_grad = value_within_block + to_end[..., None] * jnp.einsum(
        "njhd,nhde->njhe", key_blocks, back_b, preferred_element_type=jnp.float32
    )
    return (
        query_gradient.reshape(tok_rows, row_width).astype(jnp.bfloat16),
        key_grad.reshape(tok_rows, row_width).astype(jnp.bfloat16),
        value_grad.reshape(tok_rows, row_width).astype(jnp.bfloat16),
    )


def solution(mesh):
    seq_ranks = mesh.shape["seq"]
    head_ranks = mesh.shape["head"]
    row_ranks = ROW if seq_ranks % ROW == 0 else 1
    col_ranks = seq_ranks // row_ranks
    grid = Mesh(mesh.devices.reshape(col_ranks, row_ranks, head_ranks), ("sz", "sx", "head"))

    def body(queries, key_rows, value_rows, out_grad, log_decay):
        return shards(
            queries, key_rows, value_rows, out_grad, log_decay, row_ranks, col_ranks, head_ranks
        )

    rows = P(("sz", "sx"), "head")
    return jax.shard_map(
        body,
        mesh=grid,
        in_specs=(rows, rows, rows, rows, P("head", ("sz", "sx"))),
        out_specs=(rows, rows, rows),
        check_vma=False,
    )
```

```python
import jax
import jax.numpy as jnp
from jax import lax
from jax.sharding import Mesh, PartitionSpec as P

HEAD_COUNT = 32
DH = 128
BLOCK = 128
ROW = 4


epsilon = 1e-06
highest = lax.Precision.HIGHEST


def pack(total_row, state):
    return jnp.concatenate([state, total_row], axis=1)


def unpack(payload):
    return payload[:, -1:, :], payload[:, :-1, :]


def radix_shifts(ranks):
    return [list(range(1, ranks))]


def forward_scan(total, state, axis, ranks):
    win_a, win_b = total, state
    excl_a, excl_b = jnp.zeros_like(total), jnp.zeros_like(state)
    rounds = radix_shifts(ranks)
    for step, shifts in enumerate(rounds):
        payload = pack(win_a, win_b)
        got = [
            unpack(lax.ppermute(payload, axis, [(i, i + s) for i in range(ranks - s)]))
            for s in shifts
        ]
        last = step == len(rounds) - 1
        for got_a, got_b in got:
            excl_b = jnp.exp(excl_a) * got_b + excl_b
            excl_a = excl_a + got_a
            if not last:
                win_b = jnp.exp(win_a) * got_b + win_b
                win_a = win_a + got_a
    return excl_b


def backward_scan(total, state, axis, ranks):
    win_a, win_c = total, state
    excl_a, excl_c = jnp.zeros_like(total), jnp.zeros_like(state)
    rounds = radix_shifts(ranks)
    for step, shifts in enumerate(rounds):
        payload = pack(win_a, win_c)
        got = [
            unpack(lax.ppermute(payload, axis, [(i + s, i) for i in range(ranks - s)]))
            for s in shifts
        ]
        last = step == len(rounds) - 1
        for got_a, got_c in got:
            excl_c = excl_c + jnp.exp(excl_a) * got_c
            excl_a = excl_a + got_a
            if not last:
                win_c = win_c + jnp.exp(win_a) * got_c
                win_a = win_a + got_a
    return excl_c


def exchange(payload, axis, ranks):
    me = lax.axis_index(axis)
    got = [lax.dynamic_index_in_dim(payload, me, 0, keepdims=False)]
    for shift in range(1, ranks):
        send = lax.dynamic_index_in_dim(payload, (me + shift) % ranks, 0, keepdims=False)
        pairs = [(i, (i + shift) % ranks) for i in range(ranks)]
        got.append(lax.ppermute(send, axis, pairs))
    stacked = jnp.stack(got)
    order = (me - jnp.arange(ranks)) % ranks
    return jnp.take(stacked, order, axis=0)


def lane_rows(shard_total, width):
    return jnp.broadcast_to(shard_total[:, None, None], (shard_total.shape[0], 1, width))


def incoming_states(shard_total, shard_state, row_ranks, col_ranks):
    parts = exchange(pack(lane_rows(shard_total, shard_state.shape[2]), shard_state), "sx", row_ranks)
    part_a, part_b = unpack(parts)
    run_a = jnp.zeros_like(part_a[0])
    run_b = jnp.zeros_like(part_b[0])
    row_a, row_b = [], []
    for pos in range(row_ranks):
        row_a.append(run_a)
        row_b.append(run_b)
        run_b = jnp.exp(part_a[pos]) * run_b + part_b[pos]
        run_a = run_a + part_a[pos]
    before_row = forward_scan(run_a[None], run_b[None], "sz", col_ranks)[0]
    result = jnp.stack(
        [jnp.exp(row_a[pos]) * before_row + row_b[pos] for pos in range(row_ranks)]
    )
    return exchange(result, "sx", row_ranks)


def outgoing_states(shard_total, shard_back, row_ranks, col_ranks):
    parts = exchange(pack(lane_rows(shard_total, shard_back.shape[2]), shard_back), "sx", row_ranks)
    part_a, part_c = unpack(parts)
    run_a = jnp.zeros_like(part_a[0])
    run_c = jnp.zeros_like(part_c[0])
    row_a, row_c = [None] * row_ranks, [None] * row_ranks
    for pos in reversed(range(row_ranks)):
        row_a[pos] = run_a
        row_c[pos] = run_c
        run_c = part_c[pos] + jnp.exp(part_a[pos]) * run_c
        run_a = run_a + part_a[pos]
    after_row = backward_scan(run_a[None], run_c[None], "sz", col_ranks)[0]
    result = jnp.stack(
        [row_c[pos] + jnp.exp(row_a[pos]) * after_row for pos in range(row_ranks)]
    )
    return exchange(result, "sx", row_ranks)


def head_sum(values, ranks):
    copies = jnp.broadcast_to(values[None], (ranks,) + values.shape)
    gathered = lax.all_to_all(copies, "head", 0, 0, tiled=True)
    return jnp.sum(gathered, axis=0)


def weigh_blocks(weights, terms):
    return jnp.sum(weights[:, :, None, None] * terms, axis=0)


def mix_blocks(mix, terms):
    return jnp.stack([weigh_blocks(mix[n], terms) for n in range(mix.shape[0])])


def shards(queries, key_rows, value_rows, out_grad, log_decay, row_ranks, col_ranks, head_ranks):
    tok_rows, row_width = queries.shape
    heads_dev = log_decay.shape[0]
    head_size = row_width // heads_dev
    blocks = tok_rows // BLOCK
    total_width = HEAD_COUNT * DH
    block_shape = (blocks, BLOCK, heads_dev, head_size)
    query_block_rows = queries.reshape(block_shape)
    key_blocks = key_rows.reshape(block_shape)
    value_block_rows = value_rows.reshape(block_shape)
    grad_blocks = out_grad.reshape(block_shape)
    decay_blocks = jnp.transpose(log_decay.reshape(heads_dev, blocks, BLOCK), (1, 2, 0))
    inside_block_mask = jnp.cumsum(decay_blocks, axis=1)
    totals = inside_block_mask[:, -1, :]
    before = jnp.cumsum(totals, axis=0) - totals
    shard_total = jnp.sum(totals, axis=0)
    token_positions = jnp.arange(BLOCK)
    causal = (token_positions[:, None] >= token_positions[None, :]).astype(jnp.float32)
    within_heads = jnp.transpose(inside_block_mask, (0, 2, 1))
    exponent = within_heads[:, :, :, None] - within_heads[:, :, None, :]
    decay_mask = jnp.exp(jnp.minimum(exponent, 0.0)) * causal
    scores = jnp.einsum(
        "nihd,njhd->nhij", query_block_rows, key_blocks, preferred_element_type=jnp.float32
    )
    attention_weights = (scores * decay_mask).astype(jnp.bfloat16)
    intra_out = jnp.einsum(
        "nhij,njhd->nihd", attention_weights, value_block_rows, preferred_element_type=jnp.float32
    )
    to_end = jnp.exp(totals[:, None, :] - inside_block_mask)
    keys_scaled = (to_end[..., None] * key_blocks).astype(jnp.bfloat16)
    block_terms = jnp.einsum(
        "njhd,njhe->nhde", keys_scaled, value_block_rows, preferred_element_type=jnp.float32
    )
    block_ids = jnp.arange(blocks)
    earlier_blocks = (block_ids[:, None] > block_ids[None, :]).astype(jnp.float32)
    forward_exp = before[:, None, :] - before[None, :, :] - totals[None, :, :]
    forward_mix = jnp.exp(jnp.minimum(forward_exp, 0.0)) * earlier_blocks[:, :, None]
    local_states = mix_blocks(forward_mix, block_terms)
    shard_state = weigh_blocks(jnp.exp(shard_total[None, :] - before - totals), block_terms)
    incoming = incoming_states(shard_total, shard_state, row_ranks, col_ranks)
    states = local_states + jnp.exp(before)[:, :, None, None] * incoming[None]
    backward_state = states.astype(jnp.bfloat16)
    inter_out = jnp.einsum(
        "nihd,nhde->nihe", query_block_rows, backward_state, preferred_element_type=jnp.float32
    )
    attention_output = intra_out + jnp.exp(inside_block_mask)[..., None] * inter_out
    grad_f32 = grad_blocks.astype(jnp.float32)
    square = jnp.sum(attention_output * attention_output, axis=(2, 3))
    cross_raw = jnp.sum(grad_f32 * attention_output, axis=(2, 3))
    stats = head_sum(jnp.stack([square, cross_raw]), head_ranks)
    inv_rms = lax.rsqrt(stats[0] / total_width + epsilon)
    mean_cross = inv_rms * stats[1] / total_width
    normed = attention_output * inv_rms[:, :, None, None]
    attention_gradient = (
        inv_rms[:, :, None, None]
        * (grad_f32 - normed * mean_cross[:, :, None, None])
    ).astype(jnp.bfloat16)
    score_gradient = jnp.einsum(
        "nihe,njhe->nhij", attention_gradient, value_block_rows, preferred_element_type=jnp.float32
    )
    grad_probs = (score_gradient * decay_mask).astype(jnp.bfloat16)
    query_gradient = jnp.einsum(
        "nhij,njhd->nihd", grad_probs, key_blocks, preferred_element_type=jnp.float32
    )
    query_gradient = query_gradient + jnp.exp(inside_block_mask)[..., None] * jnp.einsum(
        "nihe,nhde->nihd", attention_gradient, backward_state, preferred_element_type=jnp.float32
    )
    key_intra = jnp.einsum(
        "nhij,nihd->njhd", grad_probs, query_block_rows, preferred_element_type=jnp.float32
    )
    value_within_block = jnp.einsum(
        "nhij,nihe->njhe", attention_weights, attention_gradient, preferred_element_type=jnp.float32
    )
    scaled_query_rows = (jnp.exp(inside_block_mask)[..., None] * query_block_rows).astype(
        jnp.bfloat16
    )
    backward_terms = jnp.einsum(
        "nihd,nihe->nhde", scaled_query_rows, attention_gradient, preferred_element_type=jnp.float32
    )
    later_blocks = (block_ids[:, None] < block_ids[None, :]).astype(jnp.float32)
    backward_exp = before[None, :, :] - before[:, None, :] - totals[:, None, :]
    backward_mix = jnp.exp(jnp.minimum(backward_exp, 0.0)) * later_blocks[:, :, None]
    local_back = mix_blocks(backward_mix, backward_terms)
    shard_back = weigh_blocks(jnp.exp(before), backward_terms)
    later_state = outgoing_states(shard_total, shard_back, row_ranks, col_ranks)
    back_states = (
        local_back
        + jnp.exp(shard_total[None, :] - before - totals)[:, :, None, None] * later_state[None]
    )
    back_b = back_states.astype(jnp.bfloat16)
    key_grad = key_intra + to_end[..., None] * jnp.einsum(
        "njhe,nhde->njhd", value_block_rows, back_b, preferred_element_type=jnp.float32
    )
    value_grad = value_within_block + to_end[..., None] * jnp.einsum(
        "njhd,nhde->njhe", key_blocks, back_b, preferred_element_type=jnp.float32
    )
    return (
        query_gradient.reshape(tok_rows, row_width).astype(jnp.bfloat16),
        key_grad.reshape(tok_rows, row_width).astype(jnp.bfloat16),
        value_grad.reshape(tok_rows, row_width).astype(jnp.bfloat16),
    )


def solution(mesh):
    seq_ranks = mesh.shape["seq"]
    head_ranks = mesh.shape["head"]
    row_ranks = ROW if seq_ranks % ROW == 0 else 1
    col_ranks = seq_ranks // row_ranks
    grid = Mesh(mesh.devices.reshape(col_ranks, row_ranks, head_ranks), ("sz", "sx", "head"))

    def body(queries, key_rows, value_rows, out_grad, log_decay):
        return shards(
            queries, key_rows, value_rows, out_grad, log_decay, row_ranks, col_ranks, head_ranks
        )

    rows = P(("sz", "sx"), "head")
    return jax.shard_map(
        body,
        mesh=grid,
        in_specs=(rows, rows, rows, rows, P("head", ("sz", "sx"))),
        out_specs=(rows, rows, rows),
        check_vma=False,
    )
```

```python
import jax
import jax.numpy as jnp
from jax import lax
from jax.sharding import Mesh, PartitionSpec as P

HEAD_COUNT = 32
DH = 128
BLOCK = 128
ROW = 4


epsilon = 1e-06
highest = lax.Precision.HIGHEST


def pack(total_row, state):
    return jnp.concatenate([state, total_row], axis=1)


def unpack(payload):
    return payload[:, -1:, :], payload[:, :-1, :]


def radix_shifts(ranks):
    rounds, width = [], 1
    while width < ranks:
        rounds.append([s for s in (width, 2 * width) if s < ranks])
        width *= 3
    return rounds


def forward_scan(total, state, axis, ranks):
    win_a, win_b = total, state
    excl_a, excl_b = jnp.zeros_like(total), jnp.zeros_like(state)
    rounds = radix_shifts(ranks)
    for step, shifts in enumerate(rounds):
        payload = pack(win_a, win_b)
        got = [
            unpack(lax.ppermute(payload, axis, [(i, i + s) for i in range(ranks - s)]))
            for s in shifts
        ]
        last = step == len(rounds) - 1
        for got_a, got_b in got:
            excl_b = jnp.exp(excl_a) * got_b + excl_b
            excl_a = excl_a + got_a
            if not last:
                win_b = jnp.exp(win_a) * got_b + win_b
                win_a = win_a + got_a
    return excl_b


def backward_scan(total, state, axis, ranks):
    win_a, win_c = total, state
    excl_a, excl_c = jnp.zeros_like(total), jnp.zeros_like(state)
    rounds = radix_shifts(ranks)
    for step, shifts in enumerate(rounds):
        payload = pack(win_a, win_c)
        got = [
            unpack(lax.ppermute(payload, axis, [(i + s, i) for i in range(ranks - s)]))
            for s in shifts
        ]
        last = step == len(rounds) - 1
        for got_a, got_c in got:
            excl_c = excl_c + jnp.exp(excl_a) * got_c
            excl_a = excl_a + got_a
            if not last:
                win_c = win_c + jnp.exp(win_a) * got_c
                win_a = win_a + got_a
    return excl_c


def exchange(payload, axis, ranks):
    return lax.all_to_all(payload, axis, 0, 0, tiled=True)


def lane_rows(shard_total, width):
    return jnp.broadcast_to(shard_total[:, None, None], (shard_total.shape[0], 1, width))


def incoming_states(shard_total, shard_state, row_ranks, col_ranks):
    parts = exchange(pack(lane_rows(shard_total, shard_state.shape[2]), shard_state), "sx", row_ranks)
    part_a, part_b = unpack(parts)
    run_a = jnp.zeros_like(part_a[0])
    run_b = jnp.zeros_like(part_b[0])
    row_a, row_b = [], []
    for pos in range(row_ranks):
        row_a.append(run_a)
        row_b.append(run_b)
        run_b = jnp.exp(part_a[pos]) * run_b + part_b[pos]
        run_a = run_a + part_a[pos]
    before_row = forward_scan(run_a[None], run_b[None], "sz", col_ranks)[0]
    result = jnp.stack(
        [jnp.exp(row_a[pos]) * before_row + row_b[pos] for pos in range(row_ranks)]
    )
    return exchange(result, "sx", row_ranks)


def outgoing_states(shard_total, shard_back, row_ranks, col_ranks):
    parts = exchange(pack(lane_rows(shard_total, shard_back.shape[2]), shard_back), "sx", row_ranks)
    part_a, part_c = unpack(parts)
    run_a = jnp.zeros_like(part_a[0])
    run_c = jnp.zeros_like(part_c[0])
    row_a, row_c = [None] * row_ranks, [None] * row_ranks
    for pos in reversed(range(row_ranks)):
        row_a[pos] = run_a
        row_c[pos] = run_c
        run_c = part_c[pos] + jnp.exp(part_a[pos]) * run_c
        run_a = run_a + part_a[pos]
    after_row = backward_scan(run_a[None], run_c[None], "sz", col_ranks)[0]
    result = jnp.stack(
        [row_c[pos] + jnp.exp(row_a[pos]) * after_row for pos in range(row_ranks)]
    )
    return exchange(result, "sx", row_ranks)


def head_sum(values, ranks):
    copies = jnp.broadcast_to(values[None], (ranks,) + values.shape)
    gathered = lax.all_to_all(copies, "head", 0, 0, tiled=True)
    return jnp.sum(gathered, axis=0)


def weigh_blocks(weights, terms):
    return jnp.sum(weights[:, :, None, None] * terms, axis=0)


def mix_blocks(mix, terms):
    return jnp.stack([weigh_blocks(mix[n], terms) for n in range(mix.shape[0])])


def shards(queries, key_rows, value_rows, out_grad, log_decay, row_ranks, col_ranks, head_ranks):
    tok_rows, row_width = queries.shape
    heads_dev = log_decay.shape[0]
    head_size = row_width // heads_dev
    blocks = tok_rows // BLOCK
    total_width = HEAD_COUNT * DH
    block_shape = (blocks, BLOCK, heads_dev, head_size)
    query_block_rows = queries.reshape(block_shape)
    key_blocks = key_rows.reshape(block_shape)
    value_block_rows = value_rows.reshape(block_shape)
    grad_blocks = out_grad.reshape(block_shape)
    decay_blocks = jnp.transpose(log_decay.reshape(heads_dev, blocks, BLOCK), (1, 2, 0))
    inside_block_mask = jnp.cumsum(decay_blocks, axis=1)
    totals = inside_block_mask[:, -1, :]
    before = jnp.cumsum(totals, axis=0) - totals
    shard_total = jnp.sum(totals, axis=0)
    token_positions = jnp.arange(BLOCK)
    causal = (token_positions[:, None] >= token_positions[None, :]).astype(jnp.float32)
    within_heads = jnp.transpose(inside_block_mask, (0, 2, 1))
    exponent = within_heads[:, :, :, None] - within_heads[:, :, None, :]
    decay_mask = jnp.exp(jnp.minimum(exponent, 0.0)) * causal
    scores = jnp.einsum(
        "nihd,njhd->nhij", query_block_rows, key_blocks, preferred_element_type=jnp.float32
    )
    attention_weights = (scores * decay_mask).astype(jnp.bfloat16)
    intra_out = jnp.einsum(
        "nhij,njhd->nihd", attention_weights, value_block_rows, preferred_element_type=jnp.float32
    )
    to_end = jnp.exp(totals[:, None, :] - inside_block_mask)
    keys_scaled = (to_end[..., None] * key_blocks).astype(jnp.bfloat16)
    block_terms = jnp.einsum(
        "njhd,njhe->nhde", keys_scaled, value_block_rows, preferred_element_type=jnp.float32
    )
    block_ids = jnp.arange(blocks)
    earlier_blocks = (block_ids[:, None] > block_ids[None, :]).astype(jnp.float32)
    forward_exp = before[:, None, :] - before[None, :, :] - totals[None, :, :]
    forward_mix = jnp.exp(jnp.minimum(forward_exp, 0.0)) * earlier_blocks[:, :, None]
    local_states = mix_blocks(forward_mix, block_terms)
    shard_state = weigh_blocks(jnp.exp(shard_total[None, :] - before - totals), block_terms)
    incoming = incoming_states(shard_total, shard_state, row_ranks, col_ranks)
    states = local_states + jnp.exp(before)[:, :, None, None] * incoming[None]
    backward_state = states.astype(jnp.bfloat16)
    inter_out = jnp.einsum(
        "nihd,nhde->nihe", query_block_rows, backward_state, preferred_element_type=jnp.float32
    )
    attention_output = intra_out + jnp.exp(inside_block_mask)[..., None] * inter_out
    grad_f32 = grad_blocks.astype(jnp.float32)
    square = jnp.sum(attention_output * attention_output, axis=(2, 3))
    cross_raw = jnp.sum(grad_f32 * attention_output, axis=(2, 3))
    stats = head_sum(jnp.stack([square, cross_raw]), head_ranks)
    inv_rms = lax.rsqrt(stats[0] / total_width + epsilon)
    mean_cross = inv_rms * stats[1] / total_width
    normed = attention_output * inv_rms[:, :, None, None]
    attention_gradient = (
        inv_rms[:, :, None, None]
        * (grad_f32 - normed * mean_cross[:, :, None, None])
    ).astype(jnp.bfloat16)
    score_gradient = jnp.einsum(
        "nihe,njhe->nhij", attention_gradient, value_block_rows, preferred_element_type=jnp.float32
    )
    grad_probs = (score_gradient * decay_mask).astype(jnp.bfloat16)
    query_gradient = jnp.einsum(
        "nhij,njhd->nihd", grad_probs, key_blocks, preferred_element_type=jnp.float32
    )
    query_gradient = query_gradient + jnp.exp(inside_block_mask)[..., None] * jnp.einsum(
        "nihe,nhde->nihd", attention_gradient, backward_state, preferred_element_type=jnp.float32
    )
    key_intra = jnp.einsum(
        "nhij,nihd->njhd", grad_probs, query_block_rows, preferred_element_type=jnp.float32
    )
    value_within_block = jnp.einsum(
        "nhij,nihe->njhe", attention_weights, attention_gradient, preferred_element_type=jnp.float32
    )
    scaled_query_rows = (jnp.exp(inside_block_mask)[..., None] * query_block_rows).astype(
        jnp.bfloat16
    )
    backward_terms = jnp.einsum(
        "nihd,nihe->nhde", scaled_query_rows, attention_gradient, preferred_element_type=jnp.float32
    )
    later_blocks = (block_ids[:, None] < block_ids[None, :]).astype(jnp.float32)
    backward_exp = before[None, :, :] - before[:, None, :] - totals[:, None, :]
    backward_mix = jnp.exp(jnp.minimum(backward_exp, 0.0)) * later_blocks[:, :, None]
    local_back = mix_blocks(backward_mix, backward_terms)
    shard_back = weigh_blocks(jnp.exp(before), backward_terms)
    later_state = outgoing_states(shard_total, shard_back, row_ranks, col_ranks)
    back_states = (
        local_back
        + jnp.exp(shard_total[None, :] - before - totals)[:, :, None, None] * later_state[None]
    )
    back_b = back_states.astype(jnp.bfloat16)
    key_grad = key_intra + to_end[..., None] * jnp.einsum(
        "njhe,nhde->njhd", value_block_rows, back_b, preferred_element_type=jnp.float32
    )
    value_grad = value_within_block + to_end[..., None] * jnp.einsum(
        "njhd,nhde->njhe", key_blocks, back_b, preferred_element_type=jnp.float32
    )
    return (
        query_gradient.reshape(tok_rows, row_width).astype(jnp.bfloat16),
        key_grad.reshape(tok_rows, row_width).astype(jnp.bfloat16),
        value_grad.reshape(tok_rows, row_width).astype(jnp.bfloat16),
    )


def solution(mesh):
    seq_ranks = mesh.shape["seq"]
    head_ranks = mesh.shape["head"]
    row_ranks = ROW if seq_ranks % ROW == 0 else 1
    col_ranks = seq_ranks // row_ranks
    grid = Mesh(mesh.devices.reshape(col_ranks, row_ranks, head_ranks), ("sz", "sx", "head"))

    def body(queries, key_rows, value_rows, out_grad, log_decay):
        return shards(
            queries, key_rows, value_rows, out_grad, log_decay, row_ranks, col_ranks, head_ranks
        )

    rows = P(("sz", "sx"), "head")
    return jax.shard_map(
        body,
        mesh=grid,
        in_specs=(rows, rows, rows, rows, P("head", ("sz", "sx"))),
        out_specs=(rows, rows, rows),
        check_vma=False,
    )
```

```python
import jax
import jax.numpy as jnp
from jax import lax
from jax.sharding import Mesh, PartitionSpec as P

HEAD_COUNT = 32
DH = 128
BLOCK = 128
ROW = 4


epsilon = 1e-06
highest = lax.Precision.HIGHEST


def pack(total_row, state):
    return jnp.concatenate([state, total_row], axis=1)


def unpack(payload):
    return payload[:, -1:, :], payload[:, :-1, :]


def radix_shifts(ranks):
    rounds, width = [], 1
    while width < ranks:
        shifts = [s for s in (width, 2 * width) if s < ranks]
        rounds.append(sorted(shifts, key=lambda s: -min(s, ranks - s)))
        width *= 3
    return rounds


def forward_scan(total, state, axis, ranks):
    win_a, win_b = total, state
    excl_a, excl_b = jnp.zeros_like(total), jnp.zeros_like(state)
    rounds = radix_shifts(ranks)
    for step, shifts in enumerate(rounds):
        payload = pack(win_a, win_b)
        sent = {
            s: unpack(lax.ppermute(payload, axis, [(i, i + s) for i in range(ranks - s)]))
            for s in shifts
        }
        got = [sent[s] for s in sorted(shifts)]
        last = step == len(rounds) - 1
        for got_a, got_b in got:
            excl_b = jnp.exp(excl_a) * got_b + excl_b
            excl_a = excl_a + got_a
            if not last:
                win_b = jnp.exp(win_a) * got_b + win_b
                win_a = win_a + got_a
    return excl_b


def backward_scan(total, state, axis, ranks):
    win_a, win_c = total, state
    excl_a, excl_c = jnp.zeros_like(total), jnp.zeros_like(state)
    rounds = radix_shifts(ranks)
    for step, shifts in enumerate(rounds):
        payload = pack(win_a, win_c)
        sent = {
            s: unpack(lax.ppermute(payload, axis, [(i + s, i) for i in range(ranks - s)]))
            for s in shifts
        }
        got = [sent[s] for s in sorted(shifts)]
        last = step == len(rounds) - 1
        for got_a, got_c in got:
            excl_c = excl_c + jnp.exp(excl_a) * got_c
            excl_a = excl_a + got_a
            if not last:
                win_c = win_c + jnp.exp(win_a) * got_c
                win_a = win_a + got_a
    return excl_c


def exchange(payload, axis, ranks):
    me = lax.axis_index(axis)
    got = [lax.dynamic_index_in_dim(payload, me, 0, keepdims=False)]
    received = {}
    for shift in sorted(range(1, ranks), key=lambda s: -min(s, ranks - s)):
        send = lax.dynamic_index_in_dim(payload, (me + shift) % ranks, 0, keepdims=False)
        pairs = [(i, (i + shift) % ranks) for i in range(ranks)]
        received[shift] = lax.ppermute(send, axis, pairs)
    got += [received[shift] for shift in range(1, ranks)]
    stacked = jnp.stack(got)
    order = (me - jnp.arange(ranks)) % ranks
    return jnp.take(stacked, order, axis=0)


def lane_rows(shard_total, width):
    return jnp.broadcast_to(shard_total[:, None, None], (shard_total.shape[0], 1, width))


def incoming_states(shard_total, shard_state, row_ranks, col_ranks):
    parts = exchange(pack(lane_rows(shard_total, shard_state.shape[2]), shard_state), "sx", row_ranks)
    part_a, part_b = unpack(parts)
    run_a = jnp.zeros_like(part_a[0])
    run_b = jnp.zeros_like(part_b[0])
    row_a, row_b = [], []
    for pos in range(row_ranks):
        row_a.append(run_a)
        row_b.append(run_b)
        run_b = jnp.exp(part_a[pos]) * run_b + part_b[pos]
        run_a = run_a + part_a[pos]
    before_row = forward_scan(run_a[None], run_b[None], "sz", col_ranks)[0]
    result = jnp.stack(
        [jnp.exp(row_a[pos]) * before_row + row_b[pos] for pos in range(row_ranks)]
    )
    return exchange(result, "sx", row_ranks)


def outgoing_states(shard_total, shard_back, row_ranks, col_ranks):
    parts = exchange(pack(lane_rows(shard_total, shard_back.shape[2]), shard_back), "sx", row_ranks)
    part_a, part_c = unpack(parts)
    run_a = jnp.zeros_like(part_a[0])
    run_c = jnp.zeros_like(part_c[0])
    row_a, row_c = [None] * row_ranks, [None] * row_ranks
    for pos in reversed(range(row_ranks)):
        row_a[pos] = run_a
        row_c[pos] = run_c
        run_c = part_c[pos] + jnp.exp(part_a[pos]) * run_c
        run_a = run_a + part_a[pos]
    after_row = backward_scan(run_a[None], run_c[None], "sz", col_ranks)[0]
    result = jnp.stack(
        [row_c[pos] + jnp.exp(row_a[pos]) * after_row for pos in range(row_ranks)]
    )
    return exchange(result, "sx", row_ranks)


def head_sum(values, ranks):
    copies = jnp.broadcast_to(values[None], (ranks,) + values.shape)
    gathered = lax.all_to_all(copies, "head", 0, 0, tiled=True)
    return jnp.sum(gathered, axis=0)


def weigh_blocks(weights, terms):
    return jnp.sum(weights[:, :, None, None] * terms, axis=0)


def mix_blocks(mix, terms):
    return jnp.stack([weigh_blocks(mix[n], terms) for n in range(mix.shape[0])])


def shards(queries, key_rows, value_rows, out_grad, log_decay, row_ranks, col_ranks, head_ranks):
    tok_rows, row_width = queries.shape
    heads_dev = log_decay.shape[0]
    head_size = row_width // heads_dev
    blocks = tok_rows // BLOCK
    total_width = HEAD_COUNT * DH
    block_shape = (blocks, BLOCK, heads_dev, head_size)
    query_block_rows = queries.reshape(block_shape)
    key_blocks = key_rows.reshape(block_shape)
    value_block_rows = value_rows.reshape(block_shape)
    grad_blocks = out_grad.reshape(block_shape)
    decay_blocks = jnp.transpose(log_decay.reshape(heads_dev, blocks, BLOCK), (1, 2, 0))
    inside_block_mask = jnp.cumsum(decay_blocks, axis=1)
    totals = inside_block_mask[:, -1, :]
    before = jnp.cumsum(totals, axis=0) - totals
    shard_total = jnp.sum(totals, axis=0)
    token_positions = jnp.arange(BLOCK)
    causal = (token_positions[:, None] >= token_positions[None, :]).astype(jnp.float32)
    within_heads = jnp.transpose(inside_block_mask, (0, 2, 1))
    exponent = within_heads[:, :, :, None] - within_heads[:, :, None, :]
    decay_mask = jnp.exp(jnp.minimum(exponent, 0.0)) * causal
    scores = jnp.einsum(
        "nihd,njhd->nhij", query_block_rows, key_blocks, preferred_element_type=jnp.float32
    )
    attention_weights = (scores * decay_mask).astype(jnp.bfloat16)
    intra_out = jnp.einsum(
        "nhij,njhd->nihd", attention_weights, value_block_rows, preferred_element_type=jnp.float32
    )
    to_end = jnp.exp(totals[:, None, :] - inside_block_mask)
    keys_scaled = (to_end[..., None] * key_blocks).astype(jnp.bfloat16)
    block_terms = jnp.einsum(
        "njhd,njhe->nhde", keys_scaled, value_block_rows, preferred_element_type=jnp.float32
    )
    block_ids = jnp.arange(blocks)
    earlier_blocks = (block_ids[:, None] > block_ids[None, :]).astype(jnp.float32)
    forward_exp = before[:, None, :] - before[None, :, :] - totals[None, :, :]
    forward_mix = jnp.exp(jnp.minimum(forward_exp, 0.0)) * earlier_blocks[:, :, None]
    local_states = mix_blocks(forward_mix, block_terms)
    shard_state = weigh_blocks(jnp.exp(shard_total[None, :] - before - totals), block_terms)
    incoming = incoming_states(shard_total, shard_state, row_ranks, col_ranks)
    states = local_states + jnp.exp(before)[:, :, None, None] * incoming[None]
    backward_state = states.astype(jnp.bfloat16)
    inter_out = jnp.einsum(
        "nihd,nhde->nihe", query_block_rows, backward_state, preferred_element_type=jnp.float32
    )
    attention_output = intra_out + jnp.exp(inside_block_mask)[..., None] * inter_out
    grad_f32 = grad_blocks.astype(jnp.float32)
    square = jnp.sum(attention_output * attention_output, axis=(2, 3))
    cross_raw = jnp.sum(grad_f32 * attention_output, axis=(2, 3))
    stats = head_sum(jnp.stack([square, cross_raw]), head_ranks)
    inv_rms = lax.rsqrt(stats[0] / total_width + epsilon)
    mean_cross = inv_rms * stats[1] / total_width
    normed = attention_output * inv_rms[:, :, None, None]
    attention_gradient = (
        inv_rms[:, :, None, None]
        * (grad_f32 - normed * mean_cross[:, :, None, None])
    ).astype(jnp.bfloat16)
    score_gradient = jnp.einsum(
        "nihe,njhe->nhij", attention_gradient, value_block_rows, preferred_element_type=jnp.float32
    )
    grad_probs = (score_gradient * decay_mask).astype(jnp.bfloat16)
    query_gradient = jnp.einsum(
        "nhij,njhd->nihd", grad_probs, key_blocks, preferred_element_type=jnp.float32
    )
    query_gradient = query_gradient + jnp.exp(inside_block_mask)[..., None] * jnp.einsum(
        "nihe,nhde->nihd", attention_gradient, backward_state, preferred_element_type=jnp.float32
    )
    key_intra = jnp.einsum(
        "nhij,nihd->njhd", grad_probs, query_block_rows, preferred_element_type=jnp.float32
    )
    value_within_block = jnp.einsum(
        "nhij,nihe->njhe", attention_weights, attention_gradient, preferred_element_type=jnp.float32
    )
    scaled_query_rows = (jnp.exp(inside_block_mask)[..., None] * query_block_rows).astype(
        jnp.bfloat16
    )
    backward_terms = jnp.einsum(
        "nihd,nihe->nhde", scaled_query_rows, attention_gradient, preferred_element_type=jnp.float32
    )
    later_blocks = (block_ids[:, None] < block_ids[None, :]).astype(jnp.float32)
    backward_exp = before[None, :, :] - before[:, None, :] - totals[:, None, :]
    backward_mix = jnp.exp(jnp.minimum(backward_exp, 0.0)) * later_blocks[:, :, None]
    local_back = mix_blocks(backward_mix, backward_terms)
    shard_back = weigh_blocks(jnp.exp(before), backward_terms)
    later_state = outgoing_states(shard_total, shard_back, row_ranks, col_ranks)
    back_states = (
        local_back
        + jnp.exp(shard_total[None, :] - before - totals)[:, :, None, None] * later_state[None]
    )
    back_b = back_states.astype(jnp.bfloat16)
    key_heads, value_heads = [], []
    for h in range(heads_dev):
        back_h = back_b[:, h]
        key_h = key_intra[:, :, h] + to_end[:, :, h, None] * jnp.einsum(
            "nje,nde->njd", value_block_rows[:, :, h], back_h, preferred_element_type=jnp.float32
        )
        value_h = value_within_block[:, :, h] + to_end[:, :, h, None] * jnp.einsum(
            "njd,nde->nje", key_blocks[:, :, h], back_h, preferred_element_type=jnp.float32
        )
        key_heads.append(key_h.reshape(tok_rows, head_size).astype(jnp.bfloat16))
        value_heads.append(value_h.reshape(tok_rows, head_size).astype(jnp.bfloat16))
    return (
        query_gradient.reshape(tok_rows, row_width).astype(jnp.bfloat16),
        jnp.concatenate(key_heads, axis=1),
        jnp.concatenate(value_heads, axis=1),
    )


def solution(mesh):
    seq_ranks = mesh.shape["seq"]
    head_ranks = mesh.shape["head"]
    row_ranks = ROW if seq_ranks % ROW == 0 else 1
    col_ranks = seq_ranks // row_ranks
    grid = Mesh(mesh.devices.reshape(col_ranks, row_ranks, head_ranks), ("sz", "sx", "head"))

    def body(queries, key_rows, value_rows, out_grad, log_decay):
        return shards(
            queries, key_rows, value_rows, out_grad, log_decay, row_ranks, col_ranks, head_ranks
        )

    rows = P(("sz", "sx"), "head")
    return jax.shard_map(
        body,
        mesh=grid,
        in_specs=(rows, rows, rows, rows, P("head", ("sz", "sx"))),
        out_specs=(rows, rows, rows),
        check_vma=False,
    )
```

```python
import jax
import jax.numpy as jnp
from jax import lax
from jax.sharding import Mesh, PartitionSpec as P

HEAD_COUNT = 32
DH = 128
BLOCK = 128
ROW = 4


epsilon = 1e-06
highest = lax.Precision.HIGHEST


def pack(total_row, state):
    return jnp.concatenate([state, total_row], axis=1)


def unpack(payload):
    return payload[:, -1:, :], payload[:, :-1, :]


def radix_shifts(ranks):
    rounds, width = [], 1
    while width < ranks:
        rounds.append([s for s in (width, 2 * width) if s < ranks])
        width *= 3
    return rounds


def forward_scan(total, state, axis, ranks):
    win_a, win_b = total, state
    excl_a, excl_b = jnp.zeros_like(total), jnp.zeros_like(state)
    rounds = radix_shifts(ranks)
    for step, shifts in enumerate(rounds):
        payload = pack(win_a, win_b)
        got = [
            unpack(lax.ppermute(payload, axis, [(i, i + s) for i in range(ranks - s)]))
            for s in shifts
        ]
        last = step == len(rounds) - 1
        for got_a, got_b in got:
            excl_b = jnp.exp(excl_a) * got_b + excl_b
            excl_a = excl_a + got_a
            if not last:
                win_b = jnp.exp(win_a) * got_b + win_b
                win_a = win_a + got_a
    return excl_b


def backward_scan(total, state, axis, ranks):
    win_a, win_c = total, state
    excl_a, excl_c = jnp.zeros_like(total), jnp.zeros_like(state)
    rounds = radix_shifts(ranks)
    for step, shifts in enumerate(rounds):
        payload = pack(win_a, win_c)
        got = [
            unpack(lax.ppermute(payload, axis, [(i + s, i) for i in range(ranks - s)]))
            for s in shifts
        ]
        last = step == len(rounds) - 1
        for got_a, got_c in got:
            excl_c = excl_c + jnp.exp(excl_a) * got_c
            excl_a = excl_a + got_a
            if not last:
                win_c = win_c + jnp.exp(win_a) * got_c
                win_a = win_a + got_a
    return excl_c


def exchange(payload, axis, ranks):
    me = lax.axis_index(axis)
    got = [lax.dynamic_index_in_dim(payload, me, 0, keepdims=False)]
    for shift in range(1, ranks):
        send = lax.dynamic_index_in_dim(payload, (me + shift) % ranks, 0, keepdims=False)
        pairs = [(i, (i + shift) % ranks) for i in range(ranks)]
        got.append(lax.ppermute(send, axis, pairs))
    turned = jnp.stack([got[(-k) % ranks] for k in range(ranks)])
    doubled = jnp.concatenate([turned, turned], axis=0)
    return lax.dynamic_slice_in_dim(doubled, ranks - me, ranks, axis=0)


def lane_rows(shard_total, width):
    return jnp.broadcast_to(shard_total[:, None, None], (shard_total.shape[0], 1, width))


def incoming_states(shard_total, shard_state, row_ranks, col_ranks):
    parts = exchange(pack(lane_rows(shard_total, shard_state.shape[2]), shard_state), "sx", row_ranks)
    part_a, part_b = unpack(parts)
    run_a = jnp.zeros_like(part_a[0])
    run_b = jnp.zeros_like(part_b[0])
    row_a, row_b = [], []
    for pos in range(row_ranks):
        row_a.append(run_a)
        row_b.append(run_b)
        run_b = jnp.exp(part_a[pos]) * run_b + part_b[pos]
        run_a = run_a + part_a[pos]
    before_row = forward_scan(run_a[None], run_b[None], "sz", col_ranks)[0]
    result = jnp.stack(
        [jnp.exp(row_a[pos]) * before_row + row_b[pos] for pos in range(row_ranks)]
    )
    return exchange(result, "sx", row_ranks)


def outgoing_states(shard_total, shard_back, row_ranks, col_ranks):
    parts = exchange(pack(lane_rows(shard_total, shard_back.shape[2]), shard_back), "sx", row_ranks)
    part_a, part_c = unpack(parts)
    run_a = jnp.zeros_like(part_a[0])
    run_c = jnp.zeros_like(part_c[0])
    row_a, row_c = [None] * row_ranks, [None] * row_ranks
    for pos in reversed(range(row_ranks)):
        row_a[pos] = run_a
        row_c[pos] = run_c
        run_c = part_c[pos] + jnp.exp(part_a[pos]) * run_c
        run_a = run_a + part_a[pos]
    after_row = backward_scan(run_a[None], run_c[None], "sz", col_ranks)[0]
    result = jnp.stack(
        [row_c[pos] + jnp.exp(row_a[pos]) * after_row for pos in range(row_ranks)]
    )
    return exchange(result, "sx", row_ranks)


def head_sum(values, ranks):
    copies = jnp.broadcast_to(values[None], (ranks,) + values.shape)
    gathered = lax.all_to_all(copies, "head", 0, 0, tiled=True)
    return jnp.sum(gathered, axis=0)


def weigh_blocks(weights, terms):
    return jnp.sum(weights[:, :, None, None] * terms, axis=0)


def mix_blocks(mix, terms):
    return jnp.stack([weigh_blocks(mix[n], terms) for n in range(mix.shape[0])])


def shards(queries, key_rows, value_rows, out_grad, log_decay, row_ranks, col_ranks, head_ranks):
    tok_rows, row_width = queries.shape
    heads_dev = log_decay.shape[0]
    head_size = row_width // heads_dev
    blocks = tok_rows // BLOCK
    total_width = HEAD_COUNT * DH
    block_shape = (blocks, BLOCK, heads_dev, head_size)
    query_block_rows = queries.reshape(block_shape)
    key_blocks = key_rows.reshape(block_shape)
    value_block_rows = value_rows.reshape(block_shape)
    grad_blocks = out_grad.reshape(block_shape)
    decay_blocks = jnp.transpose(log_decay.reshape(heads_dev, blocks, BLOCK), (1, 2, 0))
    inside_block_mask = jnp.cumsum(decay_blocks, axis=1)
    totals = inside_block_mask[:, -1, :]
    before = jnp.cumsum(totals, axis=0) - totals
    shard_total = jnp.sum(totals, axis=0)
    token_positions = jnp.arange(BLOCK)
    causal = (token_positions[:, None] >= token_positions[None, :]).astype(jnp.float32)
    within_heads = jnp.transpose(inside_block_mask, (0, 2, 1))
    exponent = within_heads[:, :, :, None] - within_heads[:, :, None, :]
    decay_mask = jnp.exp(jnp.minimum(exponent, 0.0)) * causal
    scores = jnp.einsum(
        "nihd,njhd->nhij", query_block_rows, key_blocks, preferred_element_type=jnp.float32
    )
    attention_weights = (scores * decay_mask).astype(jnp.bfloat16)
    intra_out = jnp.einsum(
        "nhij,njhd->nihd", attention_weights, value_block_rows, preferred_element_type=jnp.float32
    )
    to_end = jnp.exp(totals[:, None, :] - inside_block_mask)
    keys_scaled = (to_end[..., None] * key_blocks).astype(jnp.bfloat16)
    block_terms = jnp.einsum(
        "njhd,njhe->nhde", keys_scaled, value_block_rows, preferred_element_type=jnp.float32
    )
    block_ids = jnp.arange(blocks)
    earlier_blocks = (block_ids[:, None] > block_ids[None, :]).astype(jnp.float32)
    forward_exp = before[:, None, :] - before[None, :, :] - totals[None, :, :]
    forward_mix = jnp.exp(jnp.minimum(forward_exp, 0.0)) * earlier_blocks[:, :, None]
    local_states = mix_blocks(forward_mix, block_terms)
    shard_state = weigh_blocks(jnp.exp(shard_total[None, :] - before - totals), block_terms)
    incoming = incoming_states(shard_total, shard_state, row_ranks, col_ranks)
    states = local_states + jnp.exp(before)[:, :, None, None] * incoming[None]
    backward_state = states.astype(jnp.bfloat16)
    inter_out = jnp.einsum(
        "nihd,nhde->nihe", query_block_rows, backward_state, preferred_element_type=jnp.float32
    )
    attention_output = intra_out + jnp.exp(inside_block_mask)[..., None] * inter_out
    grad_f32 = grad_blocks.astype(jnp.float32)
    square = jnp.sum(attention_output * attention_output, axis=(2, 3))
    cross_raw = jnp.sum(grad_f32 * attention_output, axis=(2, 3))
    stats = head_sum(jnp.stack([square, cross_raw]), head_ranks)
    inv_rms = lax.rsqrt(stats[0] / total_width + epsilon)
    mean_cross = inv_rms * stats[1] / total_width
    normed = attention_output * inv_rms[:, :, None, None]
    attention_gradient = (
        inv_rms[:, :, None, None]
        * (grad_f32 - normed * mean_cross[:, :, None, None])
    ).astype(jnp.bfloat16)
    score_gradient = jnp.einsum(
        "nihe,njhe->nhij", attention_gradient, value_block_rows, preferred_element_type=jnp.float32
    )
    grad_probs = (score_gradient * decay_mask).astype(jnp.bfloat16)
    query_gradient = jnp.einsum(
        "nhij,njhd->nihd", grad_probs, key_blocks, preferred_element_type=jnp.float32
    )
    query_gradient = query_gradient + jnp.exp(inside_block_mask)[..., None] * jnp.einsum(
        "nihe,nhde->nihd", attention_gradient, backward_state, preferred_element_type=jnp.float32
    )
    key_intra = jnp.einsum(
        "nhij,nihd->njhd", grad_probs, query_block_rows, preferred_element_type=jnp.float32
    )
    value_within_block = jnp.einsum(
        "nhij,nihe->njhe", attention_weights, attention_gradient, preferred_element_type=jnp.float32
    )
    scaled_query_rows = (jnp.exp(inside_block_mask)[..., None] * query_block_rows).astype(
        jnp.bfloat16
    )
    backward_terms = jnp.einsum(
        "nihd,nihe->nhde", scaled_query_rows, attention_gradient, preferred_element_type=jnp.float32
    )
    later_blocks = (block_ids[:, None] < block_ids[None, :]).astype(jnp.float32)
    backward_exp = before[None, :, :] - before[:, None, :] - totals[:, None, :]
    backward_mix = jnp.exp(jnp.minimum(backward_exp, 0.0)) * later_blocks[:, :, None]
    local_back = mix_blocks(backward_mix, backward_terms)
    shard_back = weigh_blocks(jnp.exp(before), backward_terms)
    later_state = outgoing_states(shard_total, shard_back, row_ranks, col_ranks)
    back_states = (
        local_back
        + jnp.exp(shard_total[None, :] - before - totals)[:, :, None, None] * later_state[None]
    )
    back_b = back_states.astype(jnp.bfloat16)
    key_grad = key_intra + to_end[..., None] * jnp.einsum(
        "njhe,nhde->njhd", value_block_rows, back_b, preferred_element_type=jnp.float32
    )
    value_grad = value_within_block + to_end[..., None] * jnp.einsum(
        "njhd,nhde->njhe", key_blocks, back_b, preferred_element_type=jnp.float32
    )
    return (
        query_gradient.reshape(tok_rows, row_width).astype(jnp.bfloat16),
        key_grad.reshape(tok_rows, row_width).astype(jnp.bfloat16),
        value_grad.reshape(tok_rows, row_width).astype(jnp.bfloat16),
    )


def solution(mesh):
    seq_ranks = mesh.shape["seq"]
    head_ranks = mesh.shape["head"]
    row_ranks = ROW if seq_ranks % ROW == 0 else 1
    col_ranks = seq_ranks // row_ranks
    grid = Mesh(mesh.devices.reshape(col_ranks, row_ranks, head_ranks), ("sz", "sx", "head"))

    def body(queries, key_rows, value_rows, out_grad, log_decay):
        return shards(
            queries, key_rows, value_rows, out_grad, log_decay, row_ranks, col_ranks, head_ranks
        )

    rows = P(("sz", "sx"), "head")
    return jax.shard_map(
        body,
        mesh=grid,
        in_specs=(rows, rows, rows, rows, P("head", ("sz", "sx"))),
        out_specs=(rows, rows, rows),
        check_vma=False,
    )
```

```python
import jax
import jax.numpy as jnp
from jax import lax
from jax.sharding import Mesh, PartitionSpec as P

HEAD_COUNT = 32
DH = 128
BLOCK = 128
ROW = 4


epsilon = 1e-06
highest = lax.Precision.HIGHEST


def pack(total_row, state):
    return jnp.concatenate([state, total_row], axis=1)


def unpack(payload):
    return payload[:, -1:, :], payload[:, :-1, :]


def radix_shifts(ranks):
    rounds, width = [], 1
    while width < ranks:
        rounds.append([s for s in (width, 2 * width) if s < ranks])
        width *= 3
    return rounds


def forward_scan(total, state, axis, ranks):
    win_a, win_b = total, state
    excl_a, excl_b = jnp.zeros_like(total), jnp.zeros_like(state)
    rounds = radix_shifts(ranks)
    for step, shifts in enumerate(rounds):
        payload = pack(win_a, win_b)
        got = [
            unpack(lax.ppermute(payload, axis, [(i, i + s) for i in range(ranks - s)]))
            for s in shifts
        ]
        last = step == len(rounds) - 1
        for got_a, got_b in got:
            excl_b = jnp.exp(excl_a) * got_b + excl_b
            excl_a = excl_a + got_a
            if not last:
                win_b = jnp.exp(win_a) * got_b + win_b
                win_a = win_a + got_a
    return excl_b


def backward_scan(total, state, axis, ranks):
    win_a, win_c = total, state
    excl_a, excl_c = jnp.zeros_like(total), jnp.zeros_like(state)
    rounds = radix_shifts(ranks)
    for step, shifts in enumerate(rounds):
        payload = pack(win_a, win_c)
        got = [
            unpack(lax.ppermute(payload, axis, [(i + s, i) for i in range(ranks - s)]))
            for s in shifts
        ]
        last = step == len(rounds) - 1
        for got_a, got_c in got:
            excl_c = excl_c + jnp.exp(excl_a) * got_c
            excl_a = excl_a + got_a
            if not last:
                win_c = win_c + jnp.exp(win_a) * got_c
                win_a = win_a + got_a
    return excl_c


def exchange(payload, axis, ranks):
    me = lax.axis_index(axis)
    got = [lax.dynamic_index_in_dim(payload, me, 0, keepdims=False)]
    for shift in range(1, ranks):
        send = lax.dynamic_index_in_dim(payload, (me + shift) % ranks, 0, keepdims=False)
        pairs = [(i, (i + shift) % ranks) for i in range(ranks)]
        got.append(lax.ppermute(send, axis, pairs))
    outs = []
    for j in range(ranks):
        source = (me - j) % ranks
        pick = got[0]
        for shift in range(1, ranks):
            pick = jnp.where(source == shift, got[shift], pick)
        outs.append(pick)
    return jnp.stack(outs)


def lane_rows(shard_total, width):
    return jnp.broadcast_to(shard_total[:, None, None], (shard_total.shape[0], 1, width))


def incoming_states(shard_total, shard_state, row_ranks, col_ranks):
    parts = exchange(pack(lane_rows(shard_total, shard_state.shape[2]), shard_state), "sx", row_ranks)
    part_a, part_b = unpack(parts)
    run_a = jnp.zeros_like(part_a[0])
    run_b = jnp.zeros_like(part_b[0])
    row_a, row_b = [], []
    for pos in range(row_ranks):
        row_a.append(run_a)
        row_b.append(run_b)
        run_b = jnp.exp(part_a[pos]) * run_b + part_b[pos]
        run_a = run_a + part_a[pos]
    before_row = forward_scan(run_a[None], run_b[None], "sz", col_ranks)[0]
    result = jnp.stack(
        [jnp.exp(row_a[pos]) * before_row + row_b[pos] for pos in range(row_ranks)]
    )
    return exchange(result, "sx", row_ranks)


def outgoing_states(shard_total, shard_back, row_ranks, col_ranks):
    parts = exchange(pack(lane_rows(shard_total, shard_back.shape[2]), shard_back), "sx", row_ranks)
    part_a, part_c = unpack(parts)
    run_a = jnp.zeros_like(part_a[0])
    run_c = jnp.zeros_like(part_c[0])
    row_a, row_c = [None] * row_ranks, [None] * row_ranks
    for pos in reversed(range(row_ranks)):
        row_a[pos] = run_a
        row_c[pos] = run_c
        run_c = part_c[pos] + jnp.exp(part_a[pos]) * run_c
        run_a = run_a + part_a[pos]
    after_row = backward_scan(run_a[None], run_c[None], "sz", col_ranks)[0]
    result = jnp.stack(
        [row_c[pos] + jnp.exp(row_a[pos]) * after_row for pos in range(row_ranks)]
    )
    return exchange(result, "sx", row_ranks)


def head_sum(values, ranks):
    copies = jnp.broadcast_to(values[None], (ranks,) + values.shape)
    gathered = lax.all_to_all(copies, "head", 0, 0, tiled=True)
    return jnp.sum(gathered, axis=0)


def weigh_blocks(weights, terms):
    return jnp.sum(weights[:, :, None, None] * terms, axis=0)


def mix_blocks(mix, terms):
    return jnp.stack([weigh_blocks(mix[n], terms) for n in range(mix.shape[0])])


def shards(queries, key_rows, value_rows, out_grad, log_decay, row_ranks, col_ranks, head_ranks):
    tok_rows, row_width = queries.shape
    heads_dev = log_decay.shape[0]
    head_size = row_width // heads_dev
    blocks = tok_rows // BLOCK
    total_width = HEAD_COUNT * DH
    block_shape = (blocks, BLOCK, heads_dev, head_size)
    query_block_rows = queries.reshape(block_shape)
    key_blocks = key_rows.reshape(block_shape)
    value_block_rows = value_rows.reshape(block_shape)
    grad_blocks = out_grad.reshape(block_shape)
    decay_blocks = jnp.transpose(log_decay.reshape(heads_dev, blocks, BLOCK), (1, 2, 0))
    inside_block_mask = jnp.cumsum(decay_blocks, axis=1)
    totals = inside_block_mask[:, -1, :]
    before = jnp.cumsum(totals, axis=0) - totals
    shard_total = jnp.sum(totals, axis=0)
    token_positions = jnp.arange(BLOCK)
    causal = (token_positions[:, None] >= token_positions[None, :]).astype(jnp.float32)
    within_heads = jnp.transpose(inside_block_mask, (0, 2, 1))
    exponent = within_heads[:, :, :, None] - within_heads[:, :, None, :]
    decay_mask = jnp.exp(jnp.minimum(exponent, 0.0)) * causal
    scores = jnp.einsum(
        "nihd,njhd->nhij", query_block_rows, key_blocks, preferred_element_type=jnp.float32
    )
    attention_weights = (scores * decay_mask).astype(jnp.bfloat16)
    intra_out = jnp.einsum(
        "nhij,njhd->nihd", attention_weights, value_block_rows, preferred_element_type=jnp.float32
    )
    to_end = jnp.exp(totals[:, None, :] - inside_block_mask)
    keys_scaled = (to_end[..., None] * key_blocks).astype(jnp.bfloat16)
    block_terms = jnp.einsum(
        "njhd,njhe->nhde", keys_scaled, value_block_rows, preferred_element_type=jnp.float32
    )
    block_ids = jnp.arange(blocks)
    earlier_blocks = (block_ids[:, None] > block_ids[None, :]).astype(jnp.float32)
    forward_exp = before[:, None, :] - before[None, :, :] - totals[None, :, :]
    forward_mix = jnp.exp(jnp.minimum(forward_exp, 0.0)) * earlier_blocks[:, :, None]
    local_states = mix_blocks(forward_mix, block_terms)
    shard_state = weigh_blocks(jnp.exp(shard_total[None, :] - before - totals), block_terms)
    incoming = incoming_states(shard_total, shard_state, row_ranks, col_ranks)
    states = local_states + jnp.exp(before)[:, :, None, None] * incoming[None]
    backward_state = states.astype(jnp.bfloat16)
    inter_out = jnp.einsum(
        "nihd,nhde->nihe", query_block_rows, backward_state, preferred_element_type=jnp.float32
    )
    attention_output = intra_out + jnp.exp(inside_block_mask)[..., None] * inter_out
    grad_f32 = grad_blocks.astype(jnp.float32)
    square = jnp.sum(attention_output * attention_output, axis=(2, 3))
    cross_raw = jnp.sum(grad_f32 * attention_output, axis=(2, 3))
    stats = head_sum(jnp.stack([square, cross_raw]), head_ranks)
    inv_rms = lax.rsqrt(stats[0] / total_width + epsilon)
    mean_cross = inv_rms * stats[1] / total_width
    normed = attention_output * inv_rms[:, :, None, None]
    attention_gradient = (
        inv_rms[:, :, None, None]
        * (grad_f32 - normed * mean_cross[:, :, None, None])
    ).astype(jnp.bfloat16)
    score_gradient = jnp.einsum(
        "nihe,njhe->nhij", attention_gradient, value_block_rows, preferred_element_type=jnp.float32
    )
    grad_probs = (score_gradient * decay_mask).astype(jnp.bfloat16)
    query_gradient = jnp.einsum(
        "nhij,njhd->nihd", grad_probs, key_blocks, preferred_element_type=jnp.float32
    )
    query_gradient = query_gradient + jnp.exp(inside_block_mask)[..., None] * jnp.einsum(
        "nihe,nhde->nihd", attention_gradient, backward_state, preferred_element_type=jnp.float32
    )
    key_intra = jnp.einsum(
        "nhij,nihd->njhd", grad_probs, query_block_rows, preferred_element_type=jnp.float32
    )
    value_within_block = jnp.einsum(
        "nhij,nihe->njhe", attention_weights, attention_gradient, preferred_element_type=jnp.float32
    )
    scaled_query_rows = (jnp.exp(inside_block_mask)[..., None] * query_block_rows).astype(
        jnp.bfloat16
    )
    backward_terms = jnp.einsum(
        "nihd,nihe->nhde", scaled_query_rows, attention_gradient, preferred_element_type=jnp.float32
    )
    later_blocks = (block_ids[:, None] < block_ids[None, :]).astype(jnp.float32)
    backward_exp = before[None, :, :] - before[:, None, :] - totals[:, None, :]
    backward_mix = jnp.exp(jnp.minimum(backward_exp, 0.0)) * later_blocks[:, :, None]
    local_back = mix_blocks(backward_mix, backward_terms)
    shard_back = weigh_blocks(jnp.exp(before), backward_terms)
    later_state = outgoing_states(shard_total, shard_back, row_ranks, col_ranks)
    back_states = (
        local_back
        + jnp.exp(shard_total[None, :] - before - totals)[:, :, None, None] * later_state[None]
    )
    back_b = back_states.astype(jnp.bfloat16)
    key_grad = key_intra + to_end[..., None] * jnp.einsum(
        "njhe,nhde->njhd", value_block_rows, back_b, preferred_element_type=jnp.float32
    )
    value_grad = value_within_block + to_end[..., None] * jnp.einsum(
        "njhd,nhde->njhe", key_blocks, back_b, preferred_element_type=jnp.float32
    )
    return (
        query_gradient.reshape(tok_rows, row_width).astype(jnp.bfloat16),
        key_grad.reshape(tok_rows, row_width).astype(jnp.bfloat16),
        value_grad.reshape(tok_rows, row_width).astype(jnp.bfloat16),
    )


def solution(mesh):
    seq_ranks = mesh.shape["seq"]
    head_ranks = mesh.shape["head"]
    row_ranks = ROW if seq_ranks % ROW == 0 else 1
    col_ranks = seq_ranks // row_ranks
    grid = Mesh(mesh.devices.reshape(col_ranks, row_ranks, head_ranks), ("sz", "sx", "head"))

    def body(queries, key_rows, value_rows, out_grad, log_decay):
        return shards(
            queries, key_rows, value_rows, out_grad, log_decay, row_ranks, col_ranks, head_ranks
        )

    rows = P(("sz", "sx"), "head")
    return jax.shard_map(
        body,
        mesh=grid,
        in_specs=(rows, rows, rows, rows, P("head", ("sz", "sx"))),
        out_specs=(rows, rows, rows),
        check_vma=False,
    )
```

```python
import jax
import jax.numpy as jnp
from jax import lax
from jax.sharding import Mesh, PartitionSpec as P

HEAD_COUNT = 32
DH = 128
BLOCK = 128
ROW = 4


epsilon = 1e-06
highest = lax.Precision.HIGHEST


def pack(total_row, state):
    return jnp.concatenate([state, total_row], axis=1)


def unpack(payload):
    return payload[:, -1:, :], payload[:, :-1, :]


def radix_shifts(ranks):
    rounds, width = [], 1
    while width < ranks:
        rounds.append([s for s in (width, 2 * width) if s < ranks])
        width *= 3
    return rounds


def forward_scan(total, state, axis, ranks):
    win_a, win_b = total, state
    excl_a, excl_b = jnp.zeros_like(total), jnp.zeros_like(state)
    rounds = radix_shifts(ranks)
    for step, shifts in enumerate(rounds):
        payload = pack(win_a, win_b)
        got = [
            unpack(lax.ppermute(payload, axis, [(i, i + s) for i in range(ranks - s)]))
            for s in shifts
        ]
        last = step == len(rounds) - 1
        for got_a, got_b in got:
            excl_b = jnp.exp(excl_a) * got_b + excl_b
            excl_a = excl_a + got_a
            if not last:
                win_b = jnp.exp(win_a) * got_b + win_b
                win_a = win_a + got_a
    return excl_b


def backward_scan(total, state, axis, ranks):
    win_a, win_c = total, state
    excl_a, excl_c = jnp.zeros_like(total), jnp.zeros_like(state)
    rounds = radix_shifts(ranks)
    for step, shifts in enumerate(rounds):
        payload = pack(win_a, win_c)
        got = [
            unpack(lax.ppermute(payload, axis, [(i + s, i) for i in range(ranks - s)]))
            for s in shifts
        ]
        last = step == len(rounds) - 1
        for got_a, got_c in got:
            excl_c = excl_c + jnp.exp(excl_a) * got_c
            excl_a = excl_a + got_a
            if not last:
                win_c = win_c + jnp.exp(win_a) * got_c
                win_a = win_a + got_a
    return excl_c


def exchange(payload, axis, ranks):
    me = lax.axis_index(axis)
    def entry(index):
        pick = payload[0]
        for k in range(1, ranks):
            pick = jnp.where(index == k, payload[k], pick)
        return pick

    got = [entry(me)]
    for shift in range(1, ranks):
        send = entry((me + shift) % ranks)
        pairs = [(i, (i + shift) % ranks) for i in range(ranks)]
        got.append(lax.ppermute(send, axis, pairs))
    outs = []
    for j in range(ranks):
        source = (me - j) % ranks
        pick = got[0]
        for shift in range(1, ranks):
            pick = jnp.where(source == shift, got[shift], pick)
        outs.append(pick)
    return jnp.stack(outs)


def lane_rows(shard_total, width):
    return jnp.broadcast_to(shard_total[:, None, None], (shard_total.shape[0], 1, width))


def incoming_states(shard_total, shard_state, row_ranks, col_ranks):
    parts = exchange(pack(lane_rows(shard_total, shard_state.shape[2]), shard_state), "sx", row_ranks)
    part_a, part_b = unpack(parts)
    run_a = jnp.zeros_like(part_a[0])
    run_b = jnp.zeros_like(part_b[0])
    row_a, row_b = [], []
    for pos in range(row_ranks):
        row_a.append(run_a)
        row_b.append(run_b)
        run_b = jnp.exp(part_a[pos]) * run_b + part_b[pos]
        run_a = run_a + part_a[pos]
    before_row = forward_scan(run_a[None], run_b[None], "sz", col_ranks)[0]
    result = jnp.stack(
        [jnp.exp(row_a[pos]) * before_row + row_b[pos] for pos in range(row_ranks)]
    )
    return exchange(result, "sx", row_ranks)


def outgoing_states(shard_total, shard_back, row_ranks, col_ranks):
    parts = exchange(pack(lane_rows(shard_total, shard_back.shape[2]), shard_back), "sx", row_ranks)
    part_a, part_c = unpack(parts)
    run_a = jnp.zeros_like(part_a[0])
    run_c = jnp.zeros_like(part_c[0])
    row_a, row_c = [None] * row_ranks, [None] * row_ranks
    for pos in reversed(range(row_ranks)):
        row_a[pos] = run_a
        row_c[pos] = run_c
        run_c = part_c[pos] + jnp.exp(part_a[pos]) * run_c
        run_a = run_a + part_a[pos]
    after_row = backward_scan(run_a[None], run_c[None], "sz", col_ranks)[0]
    result = jnp.stack(
        [row_c[pos] + jnp.exp(row_a[pos]) * after_row for pos in range(row_ranks)]
    )
    return exchange(result, "sx", row_ranks)


def head_sum(values, ranks):
    copies = jnp.broadcast_to(values[None], (ranks,) + values.shape)
    gathered = lax.all_to_all(copies, "head", 0, 0, tiled=True)
    return jnp.sum(gathered, axis=0)


def weigh_blocks(weights, terms):
    return jnp.sum(weights[:, :, None, None] * terms, axis=0)


def mix_blocks(mix, terms):
    return jnp.stack([weigh_blocks(mix[n], terms) for n in range(mix.shape[0])])


def shards(queries, key_rows, value_rows, out_grad, log_decay, row_ranks, col_ranks, head_ranks):
    tok_rows, row_width = queries.shape
    heads_dev = log_decay.shape[0]
    head_size = row_width // heads_dev
    blocks = tok_rows // BLOCK
    total_width = HEAD_COUNT * DH
    block_shape = (blocks, BLOCK, heads_dev, head_size)
    query_block_rows = queries.reshape(block_shape)
    key_blocks = key_rows.reshape(block_shape)
    value_block_rows = value_rows.reshape(block_shape)
    grad_blocks = out_grad.reshape(block_shape)
    decay_blocks = jnp.transpose(log_decay.reshape(heads_dev, blocks, BLOCK), (1, 2, 0))
    inside_block_mask = jnp.cumsum(decay_blocks, axis=1)
    totals = inside_block_mask[:, -1, :]
    before = jnp.cumsum(totals, axis=0) - totals
    shard_total = jnp.sum(totals, axis=0)
    token_positions = jnp.arange(BLOCK)
    causal = (token_positions[:, None] >= token_positions[None, :]).astype(jnp.float32)
    within_heads = jnp.transpose(inside_block_mask, (0, 2, 1))
    exponent = within_heads[:, :, :, None] - within_heads[:, :, None, :]
    decay_mask = jnp.exp(jnp.minimum(exponent, 0.0)) * causal
    scores = jnp.einsum(
        "nihd,njhd->nhij", query_block_rows, key_blocks, preferred_element_type=jnp.float32
    )
    attention_weights = (scores * decay_mask).astype(jnp.bfloat16)
    intra_out = jnp.einsum(
        "nhij,njhd->nihd", attention_weights, value_block_rows, preferred_element_type=jnp.float32
    )
    to_end = jnp.exp(totals[:, None, :] - inside_block_mask)
    keys_scaled = (to_end[..., None] * key_blocks).astype(jnp.bfloat16)
    block_terms = jnp.einsum(
        "njhd,njhe->nhde", keys_scaled, value_block_rows, preferred_element_type=jnp.float32
    )
    block_ids = jnp.arange(blocks)
    earlier_blocks = (block_ids[:, None] > block_ids[None, :]).astype(jnp.float32)
    forward_exp = before[:, None, :] - before[None, :, :] - totals[None, :, :]
    forward_mix = jnp.exp(jnp.minimum(forward_exp, 0.0)) * earlier_blocks[:, :, None]
    local_states = mix_blocks(forward_mix, block_terms)
    shard_state = weigh_blocks(jnp.exp(shard_total[None, :] - before - totals), block_terms)
    incoming = incoming_states(shard_total, shard_state, row_ranks, col_ranks)
    states = local_states + jnp.exp(before)[:, :, None, None] * incoming[None]
    backward_state = states.astype(jnp.bfloat16)
    inter_out = jnp.einsum(
        "nihd,nhde->nihe", query_block_rows, backward_state, preferred_element_type=jnp.float32
    )
    attention_output = intra_out + jnp.exp(inside_block_mask)[..., None] * inter_out
    grad_f32 = grad_blocks.astype(jnp.float32)
    square = jnp.sum(attention_output * attention_output, axis=(2, 3))
    cross_raw = jnp.sum(grad_f32 * attention_output, axis=(2, 3))
    stats = head_sum(jnp.stack([square, cross_raw]), head_ranks)
    inv_rms = lax.rsqrt(stats[0] / total_width + epsilon)
    mean_cross = inv_rms * stats[1] / total_width
    normed = attention_output * inv_rms[:, :, None, None]
    attention_gradient = (
        inv_rms[:, :, None, None]
        * (grad_f32 - normed * mean_cross[:, :, None, None])
    ).astype(jnp.bfloat16)
    score_gradient = jnp.einsum(
        "nihe,njhe->nhij", attention_gradient, value_block_rows, preferred_element_type=jnp.float32
    )
    grad_probs = (score_gradient * decay_mask).astype(jnp.bfloat16)
    query_gradient = jnp.einsum(
        "nhij,njhd->nihd", grad_probs, key_blocks, preferred_element_type=jnp.float32
    )
    query_gradient = query_gradient + jnp.exp(inside_block_mask)[..., None] * jnp.einsum(
        "nihe,nhde->nihd", attention_gradient, backward_state, preferred_element_type=jnp.float32
    )
    key_intra = jnp.einsum(
        "nhij,nihd->njhd", grad_probs, query_block_rows, preferred_element_type=jnp.float32
    )
    value_within_block = jnp.einsum(
        "nhij,nihe->njhe", attention_weights, attention_gradient, preferred_element_type=jnp.float32
    )
    scaled_query_rows = (jnp.exp(inside_block_mask)[..., None] * query_block_rows).astype(
        jnp.bfloat16
    )
    backward_terms = jnp.einsum(
        "nihd,nihe->nhde", scaled_query_rows, attention_gradient, preferred_element_type=jnp.float32
    )
    later_blocks = (block_ids[:, None] < block_ids[None, :]).astype(jnp.float32)
    backward_exp = before[None, :, :] - before[:, None, :] - totals[:, None, :]
    backward_mix = jnp.exp(jnp.minimum(backward_exp, 0.0)) * later_blocks[:, :, None]
    local_back = mix_blocks(backward_mix, backward_terms)
    shard_back = weigh_blocks(jnp.exp(before), backward_terms)
    later_state = outgoing_states(shard_total, shard_back, row_ranks, col_ranks)
    back_states = (
        local_back
        + jnp.exp(shard_total[None, :] - before - totals)[:, :, None, None] * later_state[None]
    )
    back_b = back_states.astype(jnp.bfloat16)
    key_grad = key_intra + to_end[..., None] * jnp.einsum(
        "njhe,nhde->njhd", value_block_rows, back_b, preferred_element_type=jnp.float32
    )
    value_grad = value_within_block + to_end[..., None] * jnp.einsum(
        "njhd,nhde->njhe", key_blocks, back_b, preferred_element_type=jnp.float32
    )
    return (
        query_gradient.reshape(tok_rows, row_width).astype(jnp.bfloat16),
        key_grad.reshape(tok_rows, row_width).astype(jnp.bfloat16),
        value_grad.reshape(tok_rows, row_width).astype(jnp.bfloat16),
    )


def solution(mesh):
    seq_ranks = mesh.shape["seq"]
    head_ranks = mesh.shape["head"]
    row_ranks = ROW if seq_ranks % ROW == 0 else 1
    col_ranks = seq_ranks // row_ranks
    grid = Mesh(mesh.devices.reshape(col_ranks, row_ranks, head_ranks), ("sz", "sx", "head"))

    def body(queries, key_rows, value_rows, out_grad, log_decay):
        return shards(
            queries, key_rows, value_rows, out_grad, log_decay, row_ranks, col_ranks, head_ranks
        )

    rows = P(("sz", "sx"), "head")
    return jax.shard_map(
        body,
        mesh=grid,
        in_specs=(rows, rows, rows, rows, P("head", ("sz", "sx"))),
        out_specs=(rows, rows, rows),
        check_vma=False,
    )
```

```python
import jax
import jax.numpy as jnp
from jax import lax
from jax.sharding import Mesh, PartitionSpec as P

HEAD_COUNT = 32
DH = 128
BLOCK = 128
ROW = 4


epsilon = 1e-06
highest = lax.Precision.HIGHEST


def pack(total_row, state):
    return jnp.concatenate([state, total_row], axis=1)


def unpack(payload):
    return payload[:, -1:, :], payload[:, :-1, :]


def radix_shifts(ranks):
    rounds, width = [], 1
    while width < ranks:
        rounds.append([s for s in (width, 2 * width) if s < ranks])
        width *= 3
    return rounds


def doubling_shifts(ranks):
    rounds, width = [], 1
    while width < ranks:
        rounds.append([width])
        width *= 2
    return rounds


def forward_scan(total, state, axis, ranks):
    win_a, win_b = total, state
    excl_a, excl_b = jnp.zeros_like(total), jnp.zeros_like(state)
    rounds = radix_shifts(ranks)
    for step, shifts in enumerate(rounds):
        payload = pack(win_a, win_b)
        got = [
            unpack(lax.ppermute(payload, axis, [(i, i + s) for i in range(ranks - s)]))
            for s in shifts
        ]
        last = step == len(rounds) - 1
        for got_a, got_b in got:
            excl_b = jnp.exp(excl_a) * got_b + excl_b
            excl_a = excl_a + got_a
            if not last:
                win_b = jnp.exp(win_a) * got_b + win_b
                win_a = win_a + got_a
    return excl_b


def backward_scan(total, state, axis, ranks):
    win_a, win_c = total, state
    excl_a, excl_c = jnp.zeros_like(total), jnp.zeros_like(state)
    rounds = doubling_shifts(ranks)
    for step, shifts in enumerate(rounds):
        payload = pack(win_a, win_c)
        got = [
            unpack(lax.ppermute(payload, axis, [(i + s, i) for i in range(ranks - s)]))
            for s in shifts
        ]
        last = step == len(rounds) - 1
        for got_a, got_c in got:
            excl_c = excl_c + jnp.exp(excl_a) * got_c
            excl_a = excl_a + got_a
            if not last:
                win_c = win_c + jnp.exp(win_a) * got_c
                win_a = win_a + got_a
    return excl_c


def exchange(payload, axis, ranks):
    me = lax.axis_index(axis)
    got = [lax.dynamic_index_in_dim(payload, me, 0, keepdims=False)]
    for shift in range(1, ranks):
        send = lax.dynamic_index_in_dim(payload, (me + shift) % ranks, 0, keepdims=False)
        pairs = [(i, (i + shift) % ranks) for i in range(ranks)]
        got.append(lax.ppermute(send, axis, pairs))
    outs = []
    for j in range(ranks):
        source = (me - j) % ranks
        pick = got[0]
        for shift in range(1, ranks):
            pick = jnp.where(source == shift, got[shift], pick)
        outs.append(pick)
    return jnp.stack(outs)


def lane_rows(shard_total, width):
    return jnp.broadcast_to(shard_total[:, None, None], (shard_total.shape[0], 1, width))


def incoming_states(shard_total, shard_state, row_ranks, col_ranks):
    parts = exchange(pack(lane_rows(shard_total, shard_state.shape[2]), shard_state), "sx", row_ranks)
    part_a, part_b = unpack(parts)
    run_a = jnp.zeros_like(part_a[0])
    run_b = jnp.zeros_like(part_b[0])
    row_a, row_b = [], []
    for pos in range(row_ranks):
        row_a.append(run_a)
        row_b.append(run_b)
        run_b = jnp.exp(part_a[pos]) * run_b + part_b[pos]
        run_a = run_a + part_a[pos]
    before_row = forward_scan(run_a[None], run_b[None], "sz", col_ranks)[0]
    result = jnp.stack(
        [jnp.exp(row_a[pos]) * before_row + row_b[pos] for pos in range(row_ranks)]
    )
    return exchange(result, "sx", row_ranks)


def outgoing_states(shard_total, shard_back, row_ranks, col_ranks):
    parts = exchange(pack(lane_rows(shard_total, shard_back.shape[2]), shard_back), "sx", row_ranks)
    part_a, part_c = unpack(parts)
    run_a = jnp.zeros_like(part_a[0])
    run_c = jnp.zeros_like(part_c[0])
    row_a, row_c = [None] * row_ranks, [None] * row_ranks
    for pos in reversed(range(row_ranks)):
        row_a[pos] = run_a
        row_c[pos] = run_c
        run_c = part_c[pos] + jnp.exp(part_a[pos]) * run_c
        run_a = run_a + part_a[pos]
    after_row = backward_scan(run_a[None], run_c[None], "sz", col_ranks)[0]
    result = jnp.stack(
        [row_c[pos] + jnp.exp(row_a[pos]) * after_row for pos in range(row_ranks)]
    )
    return exchange(result, "sx", row_ranks)


def head_sum(values, ranks):
    copies = jnp.broadcast_to(values[None], (ranks,) + values.shape)
    gathered = lax.all_to_all(copies, "head", 0, 0, tiled=True)
    return jnp.sum(gathered, axis=0)


def weigh_blocks(weights, terms):
    return jnp.sum(weights[:, :, None, None] * terms, axis=0)


def mix_blocks(mix, terms):
    return jnp.stack([weigh_blocks(mix[n], terms) for n in range(mix.shape[0])])


def shards(queries, key_rows, value_rows, out_grad, log_decay, row_ranks, col_ranks, head_ranks):
    tok_rows, row_width = queries.shape
    heads_dev = log_decay.shape[0]
    head_size = row_width // heads_dev
    blocks = tok_rows // BLOCK
    total_width = HEAD_COUNT * DH
    block_shape = (blocks, BLOCK, heads_dev, head_size)
    query_block_rows = queries.reshape(block_shape)
    key_blocks = key_rows.reshape(block_shape)
    value_block_rows = value_rows.reshape(block_shape)
    grad_blocks = out_grad.reshape(block_shape)
    decay_blocks = jnp.transpose(log_decay.reshape(heads_dev, blocks, BLOCK), (1, 2, 0))
    inside_block_mask = jnp.cumsum(decay_blocks, axis=1)
    totals = inside_block_mask[:, -1, :]
    before = jnp.cumsum(totals, axis=0) - totals
    shard_total = jnp.sum(totals, axis=0)
    token_positions = jnp.arange(BLOCK)
    causal = (token_positions[:, None] >= token_positions[None, :]).astype(jnp.float32)
    within_heads = jnp.transpose(inside_block_mask, (0, 2, 1))
    exponent = within_heads[:, :, :, None] - within_heads[:, :, None, :]
    decay_mask = jnp.exp(jnp.minimum(exponent, 0.0)) * causal
    scores = jnp.einsum(
        "nihd,njhd->nhij", query_block_rows, key_blocks, preferred_element_type=jnp.float32
    )
    attention_weights = (scores * decay_mask).astype(jnp.bfloat16)
    intra_out = jnp.einsum(
        "nhij,njhd->nihd", attention_weights, value_block_rows, preferred_element_type=jnp.float32
    )
    to_end = jnp.exp(totals[:, None, :] - inside_block_mask)
    keys_scaled = (to_end[..., None] * key_blocks).astype(jnp.bfloat16)
    block_terms = jnp.einsum(
        "njhd,njhe->nhde", keys_scaled, value_block_rows, preferred_element_type=jnp.float32
    )
    block_ids = jnp.arange(blocks)
    earlier_blocks = (block_ids[:, None] > block_ids[None, :]).astype(jnp.float32)
    forward_exp = before[:, None, :] - before[None, :, :] - totals[None, :, :]
    forward_mix = jnp.exp(jnp.minimum(forward_exp, 0.0)) * earlier_blocks[:, :, None]
    local_states = mix_blocks(forward_mix, block_terms)
    shard_state = weigh_blocks(jnp.exp(shard_total[None, :] - before - totals), block_terms)
    incoming = incoming_states(shard_total, shard_state, row_ranks, col_ranks)
    states = local_states + jnp.exp(before)[:, :, None, None] * incoming[None]
    backward_state = states.astype(jnp.bfloat16)
    inter_out = jnp.einsum(
        "nihd,nhde->nihe", query_block_rows, backward_state, preferred_element_type=jnp.float32
    )
    attention_output = intra_out + jnp.exp(inside_block_mask)[..., None] * inter_out
    grad_f32 = grad_blocks.astype(jnp.float32)
    square = jnp.sum(attention_output * attention_output, axis=(2, 3))
    cross_raw = jnp.sum(grad_f32 * attention_output, axis=(2, 3))
    stats = head_sum(jnp.stack([square, cross_raw]), head_ranks)
    inv_rms = lax.rsqrt(stats[0] / total_width + epsilon)
    mean_cross = inv_rms * stats[1] / total_width
    normed = attention_output * inv_rms[:, :, None, None]
    attention_gradient = (
        inv_rms[:, :, None, None]
        * (grad_f32 - normed * mean_cross[:, :, None, None])
    ).astype(jnp.bfloat16)
    score_gradient = jnp.einsum(
        "nihe,njhe->nhij", attention_gradient, value_block_rows, preferred_element_type=jnp.float32
    )
    grad_probs = (score_gradient * decay_mask).astype(jnp.bfloat16)
    query_gradient = jnp.einsum(
        "nhij,njhd->nihd", grad_probs, key_blocks, preferred_element_type=jnp.float32
    )
    query_gradient = query_gradient + jnp.exp(inside_block_mask)[..., None] * jnp.einsum(
        "nihe,nhde->nihd", attention_gradient, backward_state, preferred_element_type=jnp.float32
    )
    key_intra = jnp.einsum(
        "nhij,nihd->njhd", grad_probs, query_block_rows, preferred_element_type=jnp.float32
    )
    value_within_block = jnp.einsum(
        "nhij,nihe->njhe", attention_weights, attention_gradient, preferred_element_type=jnp.float32
    )
    scaled_query_rows = (jnp.exp(inside_block_mask)[..., None] * query_block_rows).astype(
        jnp.bfloat16
    )
    backward_terms = jnp.einsum(
        "nihd,nihe->nhde", scaled_query_rows, attention_gradient, preferred_element_type=jnp.float32
    )
    later_blocks = (block_ids[:, None] < block_ids[None, :]).astype(jnp.float32)
    backward_exp = before[None, :, :] - before[:, None, :] - totals[:, None, :]
    backward_mix = jnp.exp(jnp.minimum(backward_exp, 0.0)) * later_blocks[:, :, None]
    local_back = mix_blocks(backward_mix, backward_terms)
    shard_back = weigh_blocks(jnp.exp(before), backward_terms)
    later_state = outgoing_states(shard_total, shard_back, row_ranks, col_ranks)
    back_states = (
        local_back
        + jnp.exp(shard_total[None, :] - before - totals)[:, :, None, None] * later_state[None]
    )
    back_b = back_states.astype(jnp.bfloat16)
    key_grad = key_intra + to_end[..., None] * jnp.einsum(
        "njhe,nhde->njhd", value_block_rows, back_b, preferred_element_type=jnp.float32
    )
    value_grad = value_within_block + to_end[..., None] * jnp.einsum(
        "njhd,nhde->njhe", key_blocks, back_b, preferred_element_type=jnp.float32
    )
    return (
        query_gradient.reshape(tok_rows, row_width).astype(jnp.bfloat16),
        key_grad.reshape(tok_rows, row_width).astype(jnp.bfloat16),
        value_grad.reshape(tok_rows, row_width).astype(jnp.bfloat16),
    )


def solution(mesh):
    seq_ranks = mesh.shape["seq"]
    head_ranks = mesh.shape["head"]
    row_ranks = ROW if seq_ranks % ROW == 0 else 1
    col_ranks = seq_ranks // row_ranks
    grid = Mesh(mesh.devices.reshape(col_ranks, row_ranks, head_ranks), ("sz", "sx", "head"))

    def body(queries, key_rows, value_rows, out_grad, log_decay):
        return shards(
            queries, key_rows, value_rows, out_grad, log_decay, row_ranks, col_ranks, head_ranks
        )

    rows = P(("sz", "sx"), "head")
    return jax.shard_map(
        body,
        mesh=grid,
        in_specs=(rows, rows, rows, rows, P("head", ("sz", "sx"))),
        out_specs=(rows, rows, rows),
        check_vma=False,
    )
```

```python
import jax
import jax.numpy as jnp
from jax import lax
from jax.sharding import Mesh, PartitionSpec as P

HEAD_COUNT = 32
DH = 128
BLOCK = 128
ROW = 4


epsilon = 1e-06
highest = lax.Precision.HIGHEST


def pack(total_row, state):
    return jnp.concatenate([state, total_row], axis=1)


def unpack(payload):
    return payload[:, -1:, :], payload[:, :-1, :]


def radix_shifts(ranks):
    rounds, width = [], 1
    while width < ranks:
        rounds.append([s for s in (width, 2 * width) if s < ranks])
        width *= 3
    return rounds


def doubling_shifts(ranks):
    rounds, width = [], 1
    while width < ranks:
        rounds.append([width])
        width *= 2
    return rounds


def forward_scan(total, state, axis, ranks):
    win_a, win_b = total, state
    excl_a, excl_b = jnp.zeros_like(total), jnp.zeros_like(state)
    rounds = doubling_shifts(ranks)
    for step, shifts in enumerate(rounds):
        payload = pack(win_a, win_b)
        got = [
            unpack(lax.ppermute(payload, axis, [(i, i + s) for i in range(ranks - s)]))
            for s in shifts
        ]
        last = step == len(rounds) - 1
        for got_a, got_b in got:
            excl_b = jnp.exp(excl_a) * got_b + excl_b
            excl_a = excl_a + got_a
            if not last:
                win_b = jnp.exp(win_a) * got_b + win_b
                win_a = win_a + got_a
    return excl_b


def backward_scan(total, state, axis, ranks):
    win_a, win_c = total, state
    excl_a, excl_c = jnp.zeros_like(total), jnp.zeros_like(state)
    rounds = doubling_shifts(ranks)
    for step, shifts in enumerate(rounds):
        payload = pack(win_a, win_c)
        got = [
            unpack(lax.ppermute(payload, axis, [(i + s, i) for i in range(ranks - s)]))
            for s in shifts
        ]
        last = step == len(rounds) - 1
        for got_a, got_c in got:
            excl_c = excl_c + jnp.exp(excl_a) * got_c
            excl_a = excl_a + got_a
            if not last:
                win_c = win_c + jnp.exp(win_a) * got_c
                win_a = win_a + got_a
    return excl_c


def exchange(payload, axis, ranks):
    me = lax.axis_index(axis)
    got = [lax.dynamic_index_in_dim(payload, me, 0, keepdims=False)]
    for shift in range(1, ranks):
        send = lax.dynamic_index_in_dim(payload, (me + shift) % ranks, 0, keepdims=False)
        pairs = [(i, (i + shift) % ranks) for i in range(ranks)]
        got.append(lax.ppermute(send, axis, pairs))
    outs = []
    for j in range(ranks):
        source = (me - j) % ranks
        pick = got[0]
        for shift in range(1, ranks):
            pick = jnp.where(source == shift, got[shift], pick)
        outs.append(pick)
    return jnp.stack(outs)


def lane_rows(shard_total, width):
    return jnp.broadcast_to(shard_total[:, None, None], (shard_total.shape[0], 1, width))


def incoming_states(shard_total, shard_state, row_ranks, col_ranks):
    parts = exchange(pack(lane_rows(shard_total, shard_state.shape[2]), shard_state), "sx", row_ranks)
    part_a, part_b = unpack(parts)
    run_a = jnp.zeros_like(part_a[0])
    run_b = jnp.zeros_like(part_b[0])
    row_a, row_b = [], []
    for pos in range(row_ranks):
        row_a.append(run_a)
        row_b.append(run_b)
        run_b = jnp.exp(part_a[pos]) * run_b + part_b[pos]
        run_a = run_a + part_a[pos]
    before_row = forward_scan(run_a[None], run_b[None], "sz", col_ranks)[0]
    result = jnp.stack(
        [jnp.exp(row_a[pos]) * before_row + row_b[pos] for pos in range(row_ranks)]
    )
    return exchange(result, "sx", row_ranks)


def outgoing_states(shard_total, shard_back, row_ranks, col_ranks):
    parts = exchange(pack(lane_rows(shard_total, shard_back.shape[2]), shard_back), "sx", row_ranks)
    part_a, part_c = unpack(parts)
    run_a = jnp.zeros_like(part_a[0])
    run_c = jnp.zeros_like(part_c[0])
    row_a, row_c = [None] * row_ranks, [None] * row_ranks
    for pos in reversed(range(row_ranks)):
        row_a[pos] = run_a
        row_c[pos] = run_c
        run_c = part_c[pos] + jnp.exp(part_a[pos]) * run_c
        run_a = run_a + part_a[pos]
    after_row = backward_scan(run_a[None], run_c[None], "sz", col_ranks)[0]
    result = jnp.stack(
        [row_c[pos] + jnp.exp(row_a[pos]) * after_row for pos in range(row_ranks)]
    )
    return exchange(result, "sx", row_ranks)


def head_sum(values, ranks):
    copies = jnp.broadcast_to(values[None], (ranks,) + values.shape)
    gathered = lax.all_to_all(copies, "head", 0, 0, tiled=True)
    return jnp.sum(gathered, axis=0)


def weigh_blocks(weights, terms):
    return jnp.sum(weights[:, :, None, None] * terms, axis=0)


def mix_blocks(mix, terms):
    return jnp.stack([weigh_blocks(mix[n], terms) for n in range(mix.shape[0])])


def shards(queries, key_rows, value_rows, out_grad, log_decay, row_ranks, col_ranks, head_ranks):
    tok_rows, row_width = queries.shape
    heads_dev = log_decay.shape[0]
    head_size = row_width // heads_dev
    blocks = tok_rows // BLOCK
    total_width = HEAD_COUNT * DH
    block_shape = (blocks, BLOCK, heads_dev, head_size)
    query_block_rows = queries.reshape(block_shape)
    key_blocks = key_rows.reshape(block_shape)
    value_block_rows = value_rows.reshape(block_shape)
    grad_blocks = out_grad.reshape(block_shape)
    decay_blocks = jnp.transpose(log_decay.reshape(heads_dev, blocks, BLOCK), (1, 2, 0))
    inside_block_mask = jnp.cumsum(decay_blocks, axis=1)
    totals = inside_block_mask[:, -1, :]
    before = jnp.cumsum(totals, axis=0) - totals
    shard_total = jnp.sum(totals, axis=0)
    token_positions = jnp.arange(BLOCK)
    causal = (token_positions[:, None] >= token_positions[None, :]).astype(jnp.float32)
    within_heads = jnp.transpose(inside_block_mask, (0, 2, 1))
    exponent = within_heads[:, :, :, None] - within_heads[:, :, None, :]
    decay_mask = jnp.exp(jnp.minimum(exponent, 0.0)) * causal
    scores = jnp.einsum(
        "nihd,njhd->nhij", query_block_rows, key_blocks, preferred_element_type=jnp.float32
    )
    attention_weights = (scores * decay_mask).astype(jnp.bfloat16)
    intra_out = jnp.einsum(
        "nhij,njhd->nihd", attention_weights, value_block_rows, preferred_element_type=jnp.float32
    )
    to_end = jnp.exp(totals[:, None, :] - inside_block_mask)
    keys_scaled = (to_end[..., None] * key_blocks).astype(jnp.bfloat16)
    block_terms = jnp.einsum(
        "njhd,njhe->nhde", keys_scaled, value_block_rows, preferred_element_type=jnp.float32
    )
    block_ids = jnp.arange(blocks)
    earlier_blocks = (block_ids[:, None] > block_ids[None, :]).astype(jnp.float32)
    forward_exp = before[:, None, :] - before[None, :, :] - totals[None, :, :]
    forward_mix = jnp.exp(jnp.minimum(forward_exp, 0.0)) * earlier_blocks[:, :, None]
    local_states = mix_blocks(forward_mix, block_terms)
    shard_state = weigh_blocks(jnp.exp(shard_total[None, :] - before - totals), block_terms)
    incoming = incoming_states(shard_total, shard_state, row_ranks, col_ranks)
    states = local_states + jnp.exp(before)[:, :, None, None] * incoming[None]
    backward_state = states.astype(jnp.bfloat16)
    inter_out = jnp.einsum(
        "nihd,nhde->nihe", query_block_rows, backward_state, preferred_element_type=jnp.float32
    )
    attention_output = intra_out + jnp.exp(inside_block_mask)[..., None] * inter_out
    grad_f32 = grad_blocks.astype(jnp.float32)
    square = jnp.sum(attention_output * attention_output, axis=(2, 3))
    cross_raw = jnp.sum(grad_f32 * attention_output, axis=(2, 3))
    stats = head_sum(jnp.stack([square, cross_raw]), head_ranks)
    inv_rms = lax.rsqrt(stats[0] / total_width + epsilon)
    mean_cross = inv_rms * stats[1] / total_width
    normed = attention_output * inv_rms[:, :, None, None]
    attention_gradient = (
        inv_rms[:, :, None, None]
        * (grad_f32 - normed * mean_cross[:, :, None, None])
    ).astype(jnp.bfloat16)
    score_gradient = jnp.einsum(
        "nihe,njhe->nhij", attention_gradient, value_block_rows, preferred_element_type=jnp.float32
    )
    grad_probs = (score_gradient * decay_mask).astype(jnp.bfloat16)
    query_gradient = jnp.einsum(
        "nhij,njhd->nihd", grad_probs, key_blocks, preferred_element_type=jnp.float32
    )
    query_gradient = query_gradient + jnp.exp(inside_block_mask)[..., None] * jnp.einsum(
        "nihe,nhde->nihd", attention_gradient, backward_state, preferred_element_type=jnp.float32
    )
    key_intra = jnp.einsum(
        "nhij,nihd->njhd", grad_probs, query_block_rows, preferred_element_type=jnp.float32
    )
    value_within_block = jnp.einsum(
        "nhij,nihe->njhe", attention_weights, attention_gradient, preferred_element_type=jnp.float32
    )
    scaled_query_rows = (jnp.exp(inside_block_mask)[..., None] * query_block_rows).astype(
        jnp.bfloat16
    )
    backward_terms = jnp.einsum(
        "nihd,nihe->nhde", scaled_query_rows, attention_gradient, preferred_element_type=jnp.float32
    )
    later_blocks = (block_ids[:, None] < block_ids[None, :]).astype(jnp.float32)
    backward_exp = before[None, :, :] - before[:, None, :] - totals[:, None, :]
    backward_mix = jnp.exp(jnp.minimum(backward_exp, 0.0)) * later_blocks[:, :, None]
    local_back = mix_blocks(backward_mix, backward_terms)
    shard_back = weigh_blocks(jnp.exp(before), backward_terms)
    later_state = outgoing_states(shard_total, shard_back, row_ranks, col_ranks)
    back_states = (
        local_back
        + jnp.exp(shard_total[None, :] - before - totals)[:, :, None, None] * later_state[None]
    )
    back_b = back_states.astype(jnp.bfloat16)
    key_grad = key_intra + to_end[..., None] * jnp.einsum(
        "njhe,nhde->njhd", value_block_rows, back_b, preferred_element_type=jnp.float32
    )
    value_grad = value_within_block + to_end[..., None] * jnp.einsum(
        "njhd,nhde->njhe", key_blocks, back_b, preferred_element_type=jnp.float32
    )
    return (
        query_gradient.reshape(tok_rows, row_width).astype(jnp.bfloat16),
        key_grad.reshape(tok_rows, row_width).astype(jnp.bfloat16),
        value_grad.reshape(tok_rows, row_width).astype(jnp.bfloat16),
    )


def solution(mesh):
    seq_ranks = mesh.shape["seq"]
    head_ranks = mesh.shape["head"]
    row_ranks = ROW if seq_ranks % ROW == 0 else 1
    col_ranks = seq_ranks // row_ranks
    grid = Mesh(mesh.devices.reshape(col_ranks, row_ranks, head_ranks), ("sz", "sx", "head"))

    def body(queries, key_rows, value_rows, out_grad, log_decay):
        return shards(
            queries, key_rows, value_rows, out_grad, log_decay, row_ranks, col_ranks, head_ranks
        )

    rows = P(("sz", "sx"), "head")
    return jax.shard_map(
        body,
        mesh=grid,
        in_specs=(rows, rows, rows, rows, P("head", ("sz", "sx"))),
        out_specs=(rows, rows, rows),
        check_vma=False,
    )
```
